256 devices in a mesh: dp: 32 (over y, z), mp: 8 (over x, core).
Axes of the slice: x: 4, y: 4, z: 8, core: 2. Of those that a mesh axis runs over, the one named last changes fastest.
Arguments:
- hidden: bfloat16 [512, 32, 1024], P(('dp', 'mp')), may hold values from -96 to 96, as said below
- query_weight: bfloat16 [1024, 1024], P('dp', 'mp'), may hold values from -0.1875 to 0.1875
- w_key: bfloat16 [1024, 1024], P('dp', 'mp'), may hold values from -0.1875 to 0.1875
- w_value: bfloat16 [1024, 1024], P('dp', 'mp'), may hold values from -0.1875 to 0.1875
- rel_table: bfloat16 [512, 1024], P('dp'), may hold values from -6 to 6
- rel_bucket: int32 [32, 32], replicated, may hold values from 0 to 511
- w_out: bfloat16 [1024, 1024], P('mp', 'dp'), may hold values from -0.1875 to 0.1875
- w_up: bfloat16 [1024, 4096], P('dp', 'mp'), may hold values from -0.1875 to 0.1875
- w_down: bfloat16 [4096, 1024], P('mp', 'dp'), may hold values from -0.09375 to 0.09375
- w_proj: bfloat16 [1024, 128], P(('dp', 'mp')), may hold values from -0.1875 to 0.1875
- pages: bfloat16 [8192, 128, 128], P('dp'), may hold values from -0.59765625 to 0.59765625
- page_len: int32 [8192], P('dp'), may hold values from 1 to 128
- slot_per_page: int32 [8192], replicated, may hold values from 0 to 8191, as said below
- candidates: int32 [512, 16, 4], P(('dp', 'mp')), may hold values from 0 to 8191, as said below
Outputs:
- query_vectors: bfloat16 [512, 32, 128], P(('dp', 'mp'))
- scores: float32 [512, 16], P(('dp', 'mp'))
The draws below stay inside these ranges and needn't reach their ends.
Inputs may be any that keep to these rules, and one draw needn't show every extreme that they name: slot_per_page is a permutation of the slots; the page in slot s is held by index s // 256 of dp. `candidates`: among the 128 page ids of the 2 queries of one device (queries in aligned blocks of 2), at most 8 have slots held by any one index of dp, and in every such block some index of dp holds exactly 8 of them. `hidden`: token states are finite.
All inputs are finite; a program needn't handle non-finite values.
Results may differ from the reference program's by a relative error of at most 0.025.
Values may be sent and summed in bfloat16 or wider, within the bound.
No kernel may reach another device: no remote copies, remote signals or barrier semaphores. Data moves between devices by JAX's collectives and lax.ppermute only.
A program may use at most 64 MiB of HBM per device.

```python
import jax
import jax.numpy as jnp
from jax import lax

D = 1024
HEADS = 16
FF = 4096
BUCKETS = 512
HD = 64
E = 128
QLEN = 32
PTOK = 128
PPC = 4
QRY_DEV = 2
NCAND = 16
PG_DEV = 256
QUERIES = 512
PAGES = 8192
HOLDERS = 32
REQ = 128
CAP = 8


def request_tables(key):
    perm = jax.random.permutation(jax.random.fold_in(key, 11), PAGES).astype(jnp.int32)
    inverse = jnp.argsort(perm).astype(jnp.int32)
    total = HOLDERS * CAP
    dest_of = jnp.arange(total, dtype=jnp.int32) // CAP
    hot = jax.random.permutation(jax.random.fold_in(key, 12), HOLDERS)[:2].astype(jnp.int32)
    is_hot = jnp.any(dest_of[:, None] == hot[None, :], axis=1)
    keys = jax.random.split(jax.random.fold_in(key, 13), QUERIES // QRY_DEV)

    def one_block(sub):
        first, second, third = jax.random.split(sub, 3)
        noise = jax.random.randint(first, (total,), 0, 1024, dtype=jnp.int32)
        rank = jnp.where(is_hot, 0, 1 + noise) * total + jnp.arange(total, dtype=jnp.int32)
        chosen = dest_of[jnp.argsort(rank)[:REQ]]
        chosen = chosen[jax.random.permutation(second, REQ)]
        local = jax.random.randint(third, (REQ,), 0, PG_DEV, dtype=jnp.int32)
        return inverse[chosen * PG_DEV + local]
    lists = jax.vmap(one_block)(keys).reshape(QUERIES, NCAND, PPC)
    return (perm, lists.astype(jnp.int32))


def draw_slot_per_page(key, part):
    return request_tables(key)[0]


def draw_candidates(key, part):
    return request_tables(key)[1]


def draw_hidden(key, part):
    first = jax.random.fold_in(jax.random.fold_in(key, 21), 0)
    value = jnp.clip(jax.random.normal(first, (QUERIES, QLEN, D), jnp.float32), -6.0, 6.0)
    return value.astype(jnp.bfloat16)


def plant(values, own_key, smallest, top_value):
    dims = values.shape
    place = [jax.random.randint(jax.random.fold_in(own_key, axis), (), 0, dims[axis]) for axis in range(len(dims))]
    values = values.at[tuple(place)].set(smallest)
    longest = dims.index(max(dims))
    place[longest] = (place[longest] + 1) % dims[longest]
    return values.at[tuple(place)].set(top_value)


def block_scale(own_key, extent, cuts, smallest, high):
    def one(position, parts):
        draws = jax.random.uniform(jax.random.fold_in(jax.random.fold_in(own_key, 6), position), (parts,), jnp.float32, smallest / len(cuts), high / len(cuts))
        return jnp.repeat(jnp.exp(draws), extent[position] // parts).reshape((-1,) + (1,) * (len(extent) - position - 1))

    level = one(*cuts[0])
    for cut in cuts[1:]:
        level = level * one(*cut)
    return level


def centred(key, shape, spread, bound, shards=(), held_as=jnp.bfloat16):
    array = spread * jax.random.normal(key, shape, jnp.float32)
    if shards:
        array = array * block_scale(key, shape, shards, -0.22, 0.18)
    return jnp.clip(array, -bound, bound).astype(held_as)


def setup_inputs(seed: int = 0) -> dict:
    seeds = jax.random.split(jax.random.key(seed), 15)
    return {
        "hidden": draw_hidden(jax.random.fold_in(seeds[14], 71), 0),
        "query_weight": centred(seeds[1], (D, D), D ** -0.5, 0.1875, ((0, 32), (1, 8))),
        "w_key": centred(seeds[2], (D, D), D ** -0.5, 0.1875, ((0, 32), (1, 8))),
        "w_value": centred(seeds[3], (D, D), D ** -0.5, 0.1875, ((0, 32), (1, 8))),
        "rel_table": centred(seeds[4], (BUCKETS, D), 1.0, 6.0, ((0, 32),)),
        "rel_bucket": plant(jax.random.randint(seeds[5], (QLEN, QLEN), 0, BUCKETS), jax.random.fold_in(seeds[5], 1), 0, BUCKETS - 1).astype(jnp.int32),
        "w_out": centred(seeds[6], (D, D), D ** -0.5, 0.1875, ((0, 8), (1, 32))),
        "w_up": centred(seeds[7], (D, FF), D ** -0.5, 0.1875, ((0, 32), (1, 8))),
        "w_down": centred(seeds[8], (FF, D), FF ** -0.5, 0.09375, ((0, 8), (1, 32))),
        "w_proj": centred(seeds[9], (D, E), D ** -0.5, 0.1875, ((0, 256),)),
        "pages": centred(seeds[10], (PAGES, PTOK, E), 0.09, 0.59765625, ((0, 32),)),
        "page_len": plant(jax.random.randint(seeds[11], (PAGES,), 1, PTOK + 1), jax.random.fold_in(seeds[11], 1), 1, PTOK).astype(jnp.int32),
        "slot_per_page": draw_slot_per_page(jax.random.fold_in(seeds[14], 71), 0),
        "candidates": draw_candidates(jax.random.fold_in(seeds[14], 71), 0),
    }


def layer_norm(value):
    mean = lax.optimization_barrier(jnp.mean(value, axis=-1, keepdims=True))
    centered = value - mean
    var = lax.optimization_barrier(jnp.mean(centered * centered, axis=-1, keepdims=True))
    return centered / jnp.sqrt(var + 1e-07)

def reference(hidden, query_weight, w_key, w_value, rel_table, rel_bucket, w_out, w_up, w_down, w_proj, pages, page_len, slot_per_page, candidates):
    flat = hidden.reshape(QUERIES * QLEN, D)
    qx = jnp.dot(flat, query_weight, preferred_element_type=jnp.float32).astype(jnp.bfloat16)
    kx = jnp.dot(flat, w_key, preferred_element_type=jnp.float32).astype(jnp.bfloat16)
    vx = jnp.dot(flat, w_value, preferred_element_type=jnp.float32).astype(jnp.bfloat16)
    qr = jnp.dot(rel_table, query_weight, preferred_element_type=jnp.float32).astype(jnp.bfloat16)
    kr = jnp.dot(rel_table, w_key, preferred_element_type=jnp.float32).astype(jnp.bfloat16)
    qx = qx.reshape(QUERIES, QLEN, HEADS, HD)
    kx = kx.reshape(QUERIES, QLEN, HEADS, HD)
    vx = vx.reshape(QUERIES, QLEN, HEADS, HD)
    qr32 = qr.reshape(BUCKETS, HEADS, HD).astype(jnp.float32)
    key_relative_single = kr.reshape(BUCKETS, HEADS, HD).astype(jnp.float32)
    rows = jnp.arange(QLEN, dtype=jnp.int32)[:, None]
    scale = 1.0 / jnp.sqrt(jnp.float32(3 * HD))

    def attend(block):
        qone, kone, vone = block
        query_single_float = qone.astype(jnp.float32)
        k32 = kone.astype(jnp.float32)
        content = jnp.einsum('ihd,jhd->hij', query_single_float, k32)
        along_axis_name = jnp.einsum('xwe,ywe->wxy', query_single_float, key_relative_single)
        c2p = along_axis_name[:, rows, rel_bucket]
        back = jnp.einsum('jhd,bhd->hjb', k32, qr32)
        p2c = jnp.swapaxes(back[:, rows, rel_bucket], 1, 2)
        logits = (content + c2p + p2c) * scale
        probs = jax.nn.softmax(logits, axis=-1).astype(jnp.bfloat16)
        context_rows = jnp.einsum('hij,jhd->ihd', probs.astype(jnp.float32), vone.astype(jnp.float32))
        return context_rows.astype(jnp.bfloat16).reshape(QLEN, D)
    context_rows = lax.map(attend, (qx, kx, vx)).reshape(QUERIES * QLEN, D)
    attn = jnp.dot(context_rows, w_out, preferred_element_type=jnp.float32)
    mid = layer_norm(flat.astype(jnp.float32) + attn).astype(jnp.bfloat16)
    inner = jax.nn.gelu(jnp.dot(mid, w_up, preferred_element_type=jnp.float32), approximate=False).astype(jnp.bfloat16)
    mlp = jnp.dot(inner, w_down, preferred_element_type=jnp.float32)
    state = layer_norm(mid.astype(jnp.float32) + mlp).astype(jnp.bfloat16)
    proj = jnp.dot(state, w_proj, preferred_element_type=jnp.float32)
    vectors = (proj / jnp.sqrt(lax.optimization_barrier(jnp.sum(proj * proj, axis=-1, keepdims=True)) + 1e-06)).astype(jnp.bfloat16)
    vectors = vectors.reshape(QUERIES, QLEN, E)
    token_positions = jnp.arange(PTOK, dtype=jnp.int32)

    def score(block):
        vec, cand = block
        slots = slot_per_page[cand]
        chosen = pages[slots].astype(jnp.float32)
        lens = page_len[slots]
        sim = jnp.einsum('ie,cpte->cpit', vec.astype(jnp.float32), chosen)
        valid = token_positions[None, None, None, :] < lens[:, :, None, None]
        best = lax.optimization_barrier(jnp.max(jnp.where(valid, sim, -1e+30), axis=-1))
        return lax.optimization_barrier(jnp.sum(lax.optimization_barrier(jnp.max(best, axis=1)), axis=-1))
    scores = lax.map(score, (vectors, candidates))
    return (vectors, scores)
```

```python
import jax
import jax.numpy as jnp
from jax import lax
from jax.sharding import PartitionSpec as P

HD = 64


def layer_norm(value):
    mean = jnp.mean(value, axis=-1, keepdims=True)
    centered = value - mean
    var = jnp.mean(centered * centered, axis=-1, keepdims=True)
    return centered / jnp.sqrt(var + 1e-07)


def add_rows(left, piece):
    return jnp.dot(left, piece, preferred_element_type=jnp.float32)


def return_maxima(maxima):
    return lax.all_to_all(
        maxima.astype(jnp.bfloat16), "dp", split_axis=0, concat_axis=0, tiled=True
    ).astype(maxima.dtype)


def body(
    hidden,
    query_weight,
    w_key,
    w_value,
    rel_table,
    rel_bucket,
    w_out,
    w_up,
    w_down,
    w_proj,
    pages,
    page_len,
    slot_per_page,
    candidates,
):
    qry_dev, qlen, width = hidden.shape
    heads_local = query_weight.shape[1] // HD
    cols = query_weight.shape[1]
    page_owners = lax.axis_size("dp")
    n_mp = lax.axis_size("mp")

    pg_dev = pages.shape[0]
    ptok = pages.shape[1]
    ncand, ppc = (candidates.shape[1], candidates.shape[2])
    req = qry_dev * ncand * ppc
    cap = 2 * req // page_owners
    slots = slot_per_page[candidates.reshape(req)]
    dest = slots // pg_dev
    local = slots % pg_dev
    query_of = jnp.arange(req, dtype=jnp.int32) // (ncand * ppc)
    member = (dest[:, None] == jnp.arange(page_owners, dtype=jnp.int32)[None, :]).astype(jnp.int32)
    place = jnp.sum((jnp.cumsum(member, axis=0) - 1) * member, axis=1)
    index = dest * cap + place
    codes = jnp.full((page_owners * cap,), -1, jnp.int32).at[index].set(query_of * pg_dev + local)
    codes = codes.reshape(page_owners, cap)
    got = lax.all_to_all(codes, "dp", split_axis=0, concat_axis=0, tiled=True)
    where_local = got % pg_dev
    which_query = jnp.clip(got // pg_dev, 0, qry_dev - 1)
    chosen = pages[where_local]
    lens = page_len[where_local]

    w_out_t = w_out.T
    w_down_t = w_down.T
    pieces = (query_weight, w_key, w_value, w_out_t, w_up, w_down_t, rel_table, w_proj)
    flat_pieces = jnp.concatenate([p.reshape(-1) for p in pieces])
    gathered = lax.all_gather(flat_pieces, "dp", axis=0, tiled=False)
    parts = []
    start = 0
    for p in pieces:
        size = p.size
        parts.append(gathered[:, start : start + size].reshape((page_owners,) + p.shape))
        start += size
    g_q, g_k, g_v, g_out, g_up, g_down, g_rel, g_proj = parts
    wq = g_q.reshape(page_owners * query_weight.shape[0], cols)
    wk = g_k.reshape(page_owners * w_key.shape[0], cols)
    wv = g_v.reshape(page_owners * w_value.shape[0], cols)
    wo = jnp.transpose(g_out, (2, 0, 1)).reshape(w_out.shape[0], page_owners * w_out.shape[1])
    wu = g_up.reshape(page_owners * w_up.shape[0], w_up.shape[1])
    wd = jnp.transpose(g_down, (2, 0, 1)).reshape(w_down.shape[0], page_owners * w_down.shape[1])
    left_rel = g_rel.reshape(page_owners * rel_table.shape[0], rel_table.shape[1])
    proj_all = lax.all_gather(g_proj, "mp", axis=0, tiled=False)
    wp = jnp.transpose(proj_all, (1, 0, 2, 3)).reshape(page_owners * n_mp * w_proj.shape[0], w_proj.shape[1])

    tokens = lax.all_gather(hidden, "mp", axis=0, tiled=True)
    group = tokens.shape[0]
    flat = tokens.reshape(group * qlen, width)
    qsum = add_rows(flat, wq)
    ksum = add_rows(flat, wk)
    vsum = add_rows(flat, wv)
    qrsum = add_rows(left_rel, wq)
    krsum = add_rows(left_rel, wk)
    rel_q = qrsum.astype(jnp.bfloat16)
    rel_k = krsum.astype(jnp.bfloat16)
    nbuck = rel_q.shape[0]
    qx = qsum.astype(jnp.bfloat16).reshape(group, qlen, heads_local, HD)
    kx = ksum.astype(jnp.bfloat16).reshape(group, qlen, heads_local, HD)
    vx = vsum.astype(jnp.bfloat16).reshape(group, qlen, heads_local, HD)
    rel_q = rel_q.reshape(nbuck, heads_local, HD)
    rel_k = rel_k.reshape(nbuck, heads_local, HD)
    onehot = (rel_bucket[:, :, None] == jnp.arange(nbuck, dtype=jnp.int32)[None, None, :]).astype(
        jnp.float32
    )
    scale = 1.0 / jnp.sqrt(jnp.float32(3 * HD))
    content = jnp.einsum("qihd,qjhd->qhij", qx, kx, preferred_element_type=jnp.float32)
    along_axis_name = jnp.einsum("qihd,bhd->qhib", qx, rel_k, preferred_element_type=jnp.float32)
    c2p = jnp.einsum("qhib,ijb->qhij", along_axis_name, onehot, precision=lax.Precision.HIGHEST)
    back = jnp.einsum("qjhd,bhd->qhjb", kx, rel_q, preferred_element_type=jnp.float32)
    p2c = jnp.einsum("qhjb,jib->qhij", back, onehot, precision=lax.Precision.HIGHEST)
    logits = (content + c2p + p2c) * scale
    probs = jax.nn.softmax(logits, axis=-1).astype(jnp.bfloat16)
    context_rows = jnp.einsum("qhij,qjhd->qihd", probs, vx, preferred_element_type=jnp.float32)
    context_rows = context_rows.astype(jnp.bfloat16).reshape(group * qlen, cols)
    attn_terms = jnp.dot(context_rows, wo, preferred_element_type=jnp.float32)
    attn = lax.psum_scatter(
        attn_terms.astype(jnp.bfloat16), "mp", scatter_dimension=0, tiled=True
    ).astype(jnp.float32)
    own = hidden.reshape(qry_dev * qlen, width).astype(jnp.float32)
    mid = layer_norm(own + attn).astype(jnp.bfloat16)
    mid_all = lax.all_gather(mid, "mp", axis=0, tiled=True)
    up = add_rows(mid_all, wu)
    inner = jax.nn.gelu(up, approximate=False).astype(jnp.bfloat16)
    down_terms = jnp.dot(inner, wd, preferred_element_type=jnp.float32)
    mlp = lax.psum_scatter(
        down_terms.astype(jnp.bfloat16), "mp", scatter_dimension=0, tiled=True
    ).astype(jnp.float32)
    state = layer_norm(mid.astype(jnp.float32) + mlp).astype(jnp.bfloat16)
    width_out = w_proj.shape[1]
    proj = add_rows(state, wp)
    vectors = (proj / jnp.sqrt(jnp.sum(proj * proj, axis=-1, keepdims=True) + 1e-06)).astype(
        jnp.bfloat16
    )
    vectors = vectors.reshape(qry_dev, qlen, width_out)

    sent = jnp.broadcast_to(vectors[None], (page_owners, qry_dev, qlen, width_out))
    recv = lax.all_to_all(sent, "dp", split_axis=0, concat_axis=0, tiled=True)
    rows_in = jnp.take_along_axis(recv, which_query[:, :, None, None], axis=1)
    token_positions = jnp.arange(ptok, dtype=jnp.int32)
    sim = jnp.einsum("snie,snte->snit", rows_in, chosen, preferred_element_type=jnp.float32)
    valid = token_positions[None, None, None, :] < lens[:, :, None, None]
    returned = return_maxima(jnp.max(jnp.where(valid, sim, -1e30), axis=-1))
    best = returned.reshape(page_owners * cap, qlen)[index]
    best = best.reshape(qry_dev, ncand, ppc, qlen)
    scores = jnp.sum(jnp.max(best, axis=2), axis=-1)
    return (vectors, scores)


def solution(mesh):
    in_specs = (
        P(("dp", "mp"), None, None),
        P("dp", "mp"),
        P("dp", "mp"),
        P("dp", "mp"),
        P("dp", None),
        P(),
        P("mp", "dp"),
        P("dp", "mp"),
        P("mp", "dp"),
        P(("dp", "mp"), None),
        P("dp", None, None),
        P("dp"),
        P(),
        P(("dp", "mp"), None, None),
    )
    out_specs = (P(("dp", "mp"), None, None), P(("dp", "mp"), None))
    return jax.shard_map(body, mesh=mesh, in_specs=in_specs, out_specs=out_specs, check_vma=False)
```

```python
import jax
import jax.numpy as jnp
from jax import lax
from jax.sharding import PartitionSpec as P

HD = 64


def layer_norm(value):
    mean = jnp.mean(value, axis=-1, keepdims=True)
    centered = value - mean
    var = jnp.mean(centered * centered, axis=-1, keepdims=True)
    return centered / jnp.sqrt(var + 1e-07)


def add_rows(left, piece):
    return jnp.dot(left, piece, preferred_element_type=jnp.float32)


def sum_to_owner(terms, n_mp):
    pieces = terms.astype(jnp.bfloat16).reshape((n_mp, terms.shape[0] // n_mp) + terms.shape[1:])
    got = lax.all_to_all(pieces, "mp", split_axis=0, concat_axis=0, tiled=True)
    return jnp.sum(got.astype(jnp.float32), axis=0).astype(jnp.bfloat16).astype(jnp.float32)


def return_maxima(maxima):
    return lax.all_to_all(
        maxima.astype(jnp.bfloat16), "dp", split_axis=0, concat_axis=0, tiled=True
    ).astype(maxima.dtype)


def body(
    hidden,
    query_weight,
    w_key,
    w_value,
    rel_table,
    rel_bucket,
    w_out,
    w_up,
    w_down,
    w_proj,
    pages,
    page_len,
    slot_per_page,
    candidates,
):
    qry_dev, qlen, width = hidden.shape
    heads_local = query_weight.shape[1] // HD
    cols = query_weight.shape[1]
    page_owners = lax.axis_size("dp")
    n_mp = lax.axis_size("mp")

    pg_dev = pages.shape[0]
    ptok = pages.shape[1]
    ncand, ppc = (candidates.shape[1], candidates.shape[2])
    req = qry_dev * ncand * ppc
    cap = 2 * req // page_owners
    slots = slot_per_page[candidates.reshape(req)]
    dest = slots // pg_dev
    local = slots % pg_dev
    query_of = jnp.arange(req, dtype=jnp.int32) // (ncand * ppc)
    member = (dest[:, None] == jnp.arange(page_owners, dtype=jnp.int32)[None, :]).astype(jnp.int32)
    place = jnp.sum((jnp.cumsum(member, axis=0) - 1) * member, axis=1)
    index = dest * cap + place
    table_local = jnp.zeros((page_owners * cap,), jnp.int32).at[index].set(local)
    table_query = jnp.zeros((page_owners * cap,), jnp.int32).at[index].set(query_of)
    table = jnp.concatenate([table_local, table_query]).astype(jnp.bfloat16)

    w_out_t = w_out.T
    w_down_t = w_down.T
    pieces = (query_weight, w_key, w_value, w_out_t, w_up, w_down_t, rel_table, w_proj, table)
    flat_pieces = jnp.concatenate([p.reshape(-1) for p in pieces])
    gathered = lax.all_gather(flat_pieces, "dp", axis=0, tiled=False)
    parts = []
    start = 0
    for p in pieces:
        size = p.size
        parts.append(gathered[:, start : start + size].reshape((page_owners,) + p.shape))
        start += size
    g_q, g_k, g_v, g_out, g_up, g_down, g_rel, g_proj, g_table = parts
    me = lax.axis_index("dp")
    g_table = g_table.reshape(page_owners, 2, page_owners, cap)
    mine = lax.dynamic_index_in_dim(g_table, me, axis=2, keepdims=False).astype(jnp.int32)
    where_local = mine[:, 0]
    which_query = mine[:, 1]
    chosen = pages[where_local]
    lens = page_len[where_local]
    wq = g_q.reshape(page_owners * query_weight.shape[0], cols)
    wk = g_k.reshape(page_owners * w_key.shape[0], cols)
    wv = g_v.reshape(page_owners * w_value.shape[0], cols)
    wo = jnp.transpose(g_out, (2, 0, 1)).reshape(w_out.shape[0], page_owners * w_out.shape[1])
    wu = g_up.reshape(page_owners * w_up.shape[0], w_up.shape[1])
    wd = jnp.transpose(g_down, (2, 0, 1)).reshape(w_down.shape[0], page_owners * w_down.shape[1])
    left_rel = g_rel.reshape(page_owners * rel_table.shape[0], rel_table.shape[1])

    spread = jnp.broadcast_to(hidden[None], (n_mp,) + hidden.shape)
    tokens = lax.all_to_all(spread, "mp", split_axis=0, concat_axis=0, tiled=True)
    tokens = tokens.reshape((n_mp * qry_dev,) + hidden.shape[1:])
    group = tokens.shape[0]
    flat = tokens.reshape(group * qlen, width)
    qsum = add_rows(flat, wq)
    ksum = add_rows(flat, wk)
    vsum = add_rows(flat, wv)
    qrsum = add_rows(left_rel, wq)
    krsum = add_rows(left_rel, wk)
    rel_q = qrsum.astype(jnp.bfloat16)
    rel_k = krsum.astype(jnp.bfloat16)
    nbuck = rel_q.shape[0]
    qx = qsum.astype(jnp.bfloat16).reshape(group, qlen, heads_local, HD)
    kx = ksum.astype(jnp.bfloat16).reshape(group, qlen, heads_local, HD)
    vx = vsum.astype(jnp.bfloat16).reshape(group, qlen, heads_local, HD)
    rel_q = rel_q.reshape(nbuck, heads_local, HD)
    rel_k = rel_k.reshape(nbuck, heads_local, HD)
    onehot = (rel_bucket[:, :, None] == jnp.arange(nbuck, dtype=jnp.int32)[None, None, :]).astype(
        jnp.float32
    )
    scale = 1.0 / jnp.sqrt(jnp.float32(3 * HD))
    content = jnp.einsum("qihd,qjhd->qhij", qx, kx, preferred_element_type=jnp.float32)
    along_axis_name = jnp.einsum("qihd,bhd->qhib", qx, rel_k, preferred_element_type=jnp.float32)
    c2p = jnp.einsum("qhib,ijb->qhij", along_axis_name, onehot, precision=lax.Precision.HIGHEST)
    back = jnp.einsum("qjhd,bhd->qhjb", kx, rel_q, preferred_element_type=jnp.float32)
    p2c = jnp.einsum("qhjb,jib->qhij", back, onehot, precision=lax.Precision.HIGHEST)
    logits = (content + c2p + p2c) * scale
    probs = jax.nn.softmax(logits, axis=-1).astype(jnp.bfloat16)
    context_rows = jnp.einsum("qhij,qjhd->qihd", probs, vx, preferred_element_type=jnp.float32)
    context_rows = context_rows.astype(jnp.bfloat16).reshape(group * qlen, cols)
    attn_terms = jnp.dot(context_rows, wo, preferred_element_type=jnp.float32)
    attn = sum_to_owner(attn_terms, n_mp)
    own = hidden.reshape(qry_dev * qlen, width).astype(jnp.float32)
    mid = layer_norm(own + attn).astype(jnp.bfloat16)
    both = jnp.concatenate([mid.reshape(-1), g_proj.reshape(-1)])
    both_all = lax.all_gather(both, "mp", axis=0, tiled=False)
    mid_all = both_all[:, : mid.size].reshape((n_mp * mid.shape[0], mid.shape[1]))
    proj_all = both_all[:, mid.size :].reshape((n_mp,) + g_proj.shape)
    wp = jnp.transpose(proj_all, (1, 0, 2, 3)).reshape(page_owners * n_mp * w_proj.shape[0], w_proj.shape[1])
    up = add_rows(mid_all, wu)
    inner = jax.nn.gelu(up, approximate=False).astype(jnp.bfloat16)
    down_terms = jnp.dot(inner, wd, preferred_element_type=jnp.float32)
    mlp = sum_to_owner(down_terms, n_mp)
    state = layer_norm(mid.astype(jnp.float32) + mlp).astype(jnp.bfloat16)
    width_out = w_proj.shape[1]
    proj = add_rows(state, wp)
    vectors = (proj / jnp.sqrt(jnp.sum(proj * proj, axis=-1, keepdims=True) + 1e-06)).astype(
        jnp.bfloat16
    )
    vectors = vectors.reshape(qry_dev, qlen, width_out)

    sent = jnp.broadcast_to(vectors[None], (page_owners, qry_dev, qlen, width_out))
    recv = lax.all_to_all(sent, "dp", split_axis=0, concat_axis=0, tiled=True)
    rows_in = jnp.take_along_axis(recv, which_query[:, :, None, None], axis=1)
    token_positions = jnp.arange(ptok, dtype=jnp.int32)
    sim = jnp.einsum("snie,snte->snit", rows_in, chosen, preferred_element_type=jnp.float32)
    valid = token_positions[None, None, None, :] < lens[:, :, None, None]
    returned = return_maxima(jnp.max(jnp.where(valid, sim, -1e30), axis=-1))
    best = returned.reshape(page_owners * cap, qlen)[index]
    best = best.reshape(qry_dev, ncand, ppc, qlen)
    scores = jnp.sum(jnp.max(best, axis=2), axis=-1)
    return (vectors, scores)


def solution(mesh):
    in_specs = (
        P(("dp", "mp"), None, None),
        P("dp", "mp"),
        P("dp", "mp"),
        P("dp", "mp"),
        P("dp", None),
        P(),
        P("mp", "dp"),
        P("dp", "mp"),
        P("mp", "dp"),
        P(("dp", "mp"), None),
        P("dp", None, None),
        P("dp"),
        P(),
        P(("dp", "mp"), None, None),
    )
    out_specs = (P(("dp", "mp"), None, None), P(("dp", "mp"), None))
    return jax.shard_map(body, mesh=mesh, in_specs=in_specs, out_specs=out_specs, check_vma=False)
```

```python
import jax
import jax.numpy as jnp
from jax import lax
from jax.sharding import Mesh, PartitionSpec as P

HD = 64
DP = ("y", "z")
MP = ("x", "c")


def layer_norm(value):
    mean = jnp.mean(value, axis=-1, keepdims=True)
    centered = value - mean
    var = jnp.mean(centered * centered, axis=-1, keepdims=True)
    return centered / jnp.sqrt(var + 1e-07)


def add_rows(left, piece):
    return jnp.dot(left, piece, preferred_element_type=jnp.float32)


def sum_to_owner(terms, n_mp):
    pieces = terms.astype(jnp.bfloat16).reshape((n_mp, terms.shape[0] // n_mp) + terms.shape[1:])
    got = lax.all_to_all(pieces, MP, split_axis=0, concat_axis=0, tiled=True)
    return jnp.sum(got.astype(jnp.float32), axis=0).astype(jnp.bfloat16).astype(jnp.float32)


def return_maxima(maxima):
    return lax.all_to_all(
        maxima.astype(jnp.bfloat16), DP, split_axis=0, concat_axis=0, tiled=True
    ).astype(maxima.dtype)


def body(
    hidden,
    query_weight,
    w_key,
    w_value,
    rel_table,
    rel_bucket,
    w_out,
    w_up,
    w_down,
    w_proj,
    pages,
    page_len,
    slot_per_page,
    candidates,
):
    qry_dev, qlen, width = hidden.shape
    heads_local = query_weight.shape[1] // HD
    cols = query_weight.shape[1]
    page_owners = lax.axis_size(DP)
    n_mp = lax.axis_size(MP)

    pg_dev = pages.shape[0]
    ptok = pages.shape[1]
    ncand, ppc = (candidates.shape[1], candidates.shape[2])
    req = qry_dev * ncand * ppc
    cap = 2 * req // page_owners
    slots = slot_per_page[candidates.reshape(req)]
    dest = slots // pg_dev
    local = slots % pg_dev
    query_of = jnp.arange(req, dtype=jnp.int32) // (ncand * ppc)
    member = (dest[:, None] == jnp.arange(page_owners, dtype=jnp.int32)[None, :]).astype(jnp.int32)
    place = jnp.sum((jnp.cumsum(member, axis=0) - 1) * member, axis=1)
    index = dest * cap + place
    table_local = jnp.zeros((page_owners * cap,), jnp.int32).at[index].set(local)
    table_query = jnp.zeros((page_owners * cap,), jnp.int32).at[index].set(query_of)
    table = jnp.concatenate([table_local, table_query]).astype(jnp.bfloat16)

    lanes = query_weight.shape[1]
    pieces = (query_weight, w_key, w_value, w_out.T, w_up, w_down.T, rel_table, w_proj, table)
    rows = [p.size // lanes for p in pieces]
    flat_pieces = jnp.concatenate([p.reshape(-1, lanes) for p in pieces], axis=0)
    by_y = lax.all_gather(flat_pieces, DP[0], axis=0, tiled=False)
    by_zy = lax.all_gather(by_y, DP[1], axis=0, tiled=False)
    gathered = jnp.swapaxes(by_zy, 0, 1).reshape((page_owners,) + flat_pieces.shape)
    parts = []
    start = 0
    for p, n in zip(pieces, rows):
        parts.append(gathered[:, start : start + n])
        start += n
    g_q, g_k, g_v, g_out, g_up, g_down, g_rel, g_proj, g_table = parts
    me = lax.axis_index(DP)
    g_table = g_table.reshape(page_owners, 2, page_owners, cap)
    mine = lax.dynamic_index_in_dim(g_table, me, axis=2, keepdims=False).astype(jnp.int32)
    where_local = mine[:, 0]
    which_query = mine[:, 1]
    chosen = pages[where_local]
    lens = page_len[where_local]
    wq = g_q.reshape(page_owners * query_weight.shape[0], cols)
    wk = g_k.reshape(page_owners * w_key.shape[0], cols)
    wv = g_v.reshape(page_owners * w_value.shape[0], cols)
    wo = g_out.reshape(page_owners * w_out.shape[1], w_out.shape[0]).T
    wu = g_up.reshape(page_owners * w_up.shape[0], w_up.shape[1])
    wd = g_down.reshape(page_owners * w_down.shape[1], w_down.shape[0]).T
    left_rel = g_rel.reshape(page_owners * rel_table.shape[0], rel_table.shape[1])
    g_proj = g_proj.reshape((page_owners,) + w_proj.shape)

    spread = jnp.broadcast_to(hidden[None], (n_mp,) + hidden.shape)
    tokens = lax.all_to_all(spread, MP, split_axis=0, concat_axis=0, tiled=True)
    tokens = tokens.reshape((n_mp * qry_dev,) + hidden.shape[1:])
    group = tokens.shape[0]
    flat = tokens.reshape(group * qlen, width)
    qsum = add_rows(flat, wq)
    ksum = add_rows(flat, wk)
    vsum = add_rows(flat, wv)
    qrsum = add_rows(left_rel, wq)
    krsum = add_rows(left_rel, wk)
    rel_q = qrsum.astype(jnp.bfloat16)
    rel_k = krsum.astype(jnp.bfloat16)
    nbuck = rel_q.shape[0]
    qx = qsum.astype(jnp.bfloat16).reshape(group, qlen, heads_local, HD)
    kx = ksum.astype(jnp.bfloat16).reshape(group, qlen, heads_local, HD)
    vx = vsum.astype(jnp.bfloat16).reshape(group, qlen, heads_local, HD)
    rel_q = rel_q.reshape(nbuck, heads_local, HD)
    rel_k = rel_k.reshape(nbuck, heads_local, HD)
    onehot = (rel_bucket[:, :, None] == jnp.arange(nbuck, dtype=jnp.int32)[None, None, :]).astype(
        jnp.float32
    )
    scale = 1.0 / jnp.sqrt(jnp.float32(3 * HD))
    content = jnp.einsum("qihd,qjhd->qhij", qx, kx, preferred_element_type=jnp.float32)
    along_axis_name = jnp.einsum("qihd,bhd->qhib", qx, rel_k, preferred_element_type=jnp.float32)
    c2p = jnp.einsum("qhib,ijb->qhij", along_axis_name, onehot, precision=lax.Precision.HIGHEST)
    back = jnp.einsum("qjhd,bhd->qhjb", kx, rel_q, preferred_element_type=jnp.float32)
    p2c = jnp.einsum("qhjb,jib->qhij", back, onehot, precision=lax.Precision.HIGHEST)
    logits = (content + c2p + p2c) * scale
    probs = jax.nn.softmax(logits, axis=-1).astype(jnp.bfloat16)
    context_rows = jnp.einsum("qhij,qjhd->qihd", probs, vx, preferred_element_type=jnp.float32)
    context_rows = context_rows.astype(jnp.bfloat16).reshape(group * qlen, cols)
    attn_terms = jnp.dot(context_rows, wo, preferred_element_type=jnp.float32)
    attn = sum_to_owner(attn_terms, n_mp)
    own = hidden.reshape(qry_dev * qlen, width).astype(jnp.float32)
    mid = layer_norm(own + attn).astype(jnp.bfloat16)
    chosen, lens, mid = lax.optimization_barrier((chosen, lens, mid))
    both = jnp.concatenate([mid.reshape(-1), g_proj.reshape(-1)])
    both_all = lax.all_gather(both, MP, axis=0, tiled=False)
    mid_all = both_all[:, : mid.size].reshape((n_mp * mid.shape[0], mid.shape[1]))
    proj_all = both_all[:, mid.size :].reshape((n_mp,) + g_proj.shape)
    wp = jnp.transpose(proj_all, (1, 0, 2, 3)).reshape(page_owners * n_mp * w_proj.shape[0], w_proj.shape[1])
    up = add_rows(mid_all, wu)
    inner = jax.nn.gelu(up, approximate=False).astype(jnp.bfloat16)
    down_terms = jnp.dot(inner, wd, preferred_element_type=jnp.float32)
    mlp = sum_to_owner(down_terms, n_mp)
    state = layer_norm(mid.astype(jnp.float32) + mlp).astype(jnp.bfloat16)
    width_out = w_proj.shape[1]
    proj = add_rows(state, wp)
    vectors = (proj / jnp.sqrt(jnp.sum(proj * proj, axis=-1, keepdims=True) + 1e-06)).astype(
        jnp.bfloat16
    )
    vectors = vectors.reshape(qry_dev, qlen, width_out)

    sent = jnp.broadcast_to(vectors[None], (page_owners, qry_dev, qlen, width_out))
    recv = lax.all_to_all(sent, DP, split_axis=0, concat_axis=0, tiled=True)
    rows_in = jnp.take_along_axis(recv, which_query[:, :, None, None], axis=1)
    token_positions = jnp.arange(ptok, dtype=jnp.int32)
    sim = jnp.einsum("snie,snte->snit", rows_in, chosen, preferred_element_type=jnp.float32)
    valid = token_positions[None, None, None, :] < lens[:, :, None, None]
    returned = return_maxima(jnp.max(jnp.where(valid, sim, -1e30), axis=-1))
    best = returned.reshape(page_owners * cap, qlen)[index]
    best = best.reshape(qry_dev, ncand, ppc, qlen)
    scores = jnp.sum(jnp.max(best, axis=2), axis=-1)
    return (vectors, scores)


def solution(mesh):
    in_specs = (
        P(DP + MP, None, None),
        P(DP, MP),
        P(DP, MP),
        P(DP, MP),
        P(DP, None),
        P(),
        P(MP, DP),
        P(DP, MP),
        P(MP, DP),
        P(DP + MP, None),
        P(DP, None, None),
        P(DP),
        P(),
        P(DP + MP, None, None),
    )
    out_specs = (P(DP + MP, None, None), P(DP + MP, None))
    fine = Mesh(mesh.devices.reshape(mesh.devices.shape[0] // 8, 8, mesh.devices.shape[1] // 2, 2), DP + MP)
    return jax.shard_map(body, mesh=fine, in_specs=in_specs, out_specs=out_specs, check_vma=False)
```

```python
import jax
import jax.numpy as jnp
from jax import lax
from jax.sharding import Mesh, PartitionSpec as P

HD = 64
DP = ("y", "z")
MP = ("x", "c")


def layer_norm(value):
    mean = jnp.mean(value, axis=-1, keepdims=True)
    centered = value - mean
    var = jnp.mean(centered * centered, axis=-1, keepdims=True)
    return centered / jnp.sqrt(var + 1e-07)


def add_rows(left, piece):
    return jnp.dot(left, piece, preferred_element_type=jnp.float32)


def sum_to_owner(terms, n_mp):
    pieces = terms.astype(jnp.bfloat16).reshape((n_mp, terms.shape[0] // n_mp) + terms.shape[1:])
    got = lax.all_to_all(pieces, MP, split_axis=0, concat_axis=0, tiled=True)
    return jnp.sum(got.astype(jnp.float32), axis=0).astype(jnp.bfloat16).astype(jnp.float32)


def gather_rows(pieces, lanes, page_owners):
    rows = [p.size // lanes for p in pieces]
    flat_pieces = jnp.concatenate([p.reshape(-1, lanes) for p in pieces], axis=0)
    by_y = lax.all_gather(flat_pieces, DP[0], axis=0, tiled=False)
    by_zy = lax.all_gather(by_y, DP[1], axis=0, tiled=False)
    gathered = jnp.swapaxes(by_zy, 0, 1).reshape((page_owners,) + flat_pieces.shape)
    parts = []
    start = 0
    for n in rows:
        parts.append(gathered[:, start : start + n])
        start += n
    return parts


def return_maxima(maxima):
    return lax.all_to_all(
        maxima.astype(jnp.bfloat16), DP, split_axis=0, concat_axis=0, tiled=True
    ).astype(maxima.dtype)


def body(
    hidden,
    query_weight,
    w_key,
    w_value,
    rel_table,
    rel_bucket,
    w_out,
    w_up,
    w_down,
    w_proj,
    pages,
    page_len,
    slot_per_page,
    candidates,
):
    qry_dev, qlen, width = hidden.shape
    heads_local = query_weight.shape[1] // HD
    cols = query_weight.shape[1]
    page_owners = lax.axis_size(DP)
    n_mp = lax.axis_size(MP)

    pg_dev = pages.shape[0]
    ptok = pages.shape[1]
    ncand, ppc = (candidates.shape[1], candidates.shape[2])
    req = qry_dev * ncand * ppc
    cap = 2 * req // page_owners
    slots = slot_per_page[candidates.reshape(req)]
    dest = slots // pg_dev
    local = slots % pg_dev
    query_of = jnp.arange(req, dtype=jnp.int32) // (ncand * ppc)
    member = (dest[:, None] == jnp.arange(page_owners, dtype=jnp.int32)[None, :]).astype(jnp.int32)
    place = jnp.sum((jnp.cumsum(member, axis=0) - 1) * member, axis=1)
    index = dest * cap + place
    table_local = jnp.zeros((page_owners * cap,), jnp.int32).at[index].set(local)
    table_query = jnp.zeros((page_owners * cap,), jnp.int32).at[index].set(query_of)
    table = jnp.concatenate([table_local, table_query]).astype(jnp.bfloat16)

    lanes = query_weight.shape[1]
    first = (query_weight, w_key, w_value, w_out.T, rel_table, w_proj, table)
    second = (w_up, w_down.T)
    g_q, g_k, g_v, g_out, g_rel, g_proj, g_table = gather_rows(first, lanes, page_owners)
    g_up, g_down = gather_rows(second, lanes, page_owners)
    me = lax.axis_index(DP)
    g_table = g_table.reshape(page_owners, 2, page_owners, cap)
    mine = lax.dynamic_index_in_dim(g_table, me, axis=2, keepdims=False).astype(jnp.int32)
    where_local = mine[:, 0]
    which_query = mine[:, 1]
    chosen = pages[where_local]
    lens = page_len[where_local]
    wq = g_q.reshape(page_owners * query_weight.shape[0], cols)
    wk = g_k.reshape(page_owners * w_key.shape[0], cols)
    wv = g_v.reshape(page_owners * w_value.shape[0], cols)
    wo = g_out.reshape(page_owners * w_out.shape[1], w_out.shape[0]).T
    wu = g_up.reshape(page_owners * w_up.shape[0], w_up.shape[1])
    wd = g_down.reshape(page_owners * w_down.shape[1], w_down.shape[0]).T
    left_rel = g_rel.reshape(page_owners * rel_table.shape[0], rel_table.shape[1])
    g_proj = g_proj.reshape((page_owners,) + w_proj.shape)

    spread = jnp.broadcast_to(hidden[None], (n_mp,) + hidden.shape)
    tokens = lax.all_to_all(spread, MP, split_axis=0, concat_axis=0, tiled=True)
    tokens = tokens.reshape((n_mp * qry_dev,) + hidden.shape[1:])
    group = tokens.shape[0]
    flat = tokens.reshape(group * qlen, width)
    qsum = add_rows(flat, wq)
    ksum = add_rows(flat, wk)
    vsum = add_rows(flat, wv)
    qrsum = add_rows(left_rel, wq)
    krsum = add_rows(left_rel, wk)
    rel_q = qrsum.astype(jnp.bfloat16)
    rel_k = krsum.astype(jnp.bfloat16)
    nbuck = rel_q.shape[0]
    qx = qsum.astype(jnp.bfloat16).reshape(group, qlen, heads_local, HD)
    kx = ksum.astype(jnp.bfloat16).reshape(group, qlen, heads_local, HD)
    vx = vsum.astype(jnp.bfloat16).reshape(group, qlen, heads_local, HD)
    rel_q = rel_q.reshape(nbuck, heads_local, HD)
    rel_k = rel_k.reshape(nbuck, heads_local, HD)
    onehot = (rel_bucket[:, :, None] == jnp.arange(nbuck, dtype=jnp.int32)[None, None, :]).astype(
        jnp.float32
    )
    scale = 1.0 / jnp.sqrt(jnp.float32(3 * HD))
    content = jnp.einsum("qihd,qjhd->qhij", qx, kx, preferred_element_type=jnp.float32)
    along_axis_name = jnp.einsum("qihd,bhd->qhib", qx, rel_k, preferred_element_type=jnp.float32)
    c2p = jnp.einsum("qhib,ijb->qhij", along_axis_name, onehot, precision=lax.Precision.HIGHEST)
    back = jnp.einsum("qjhd,bhd->qhjb", kx, rel_q, preferred_element_type=jnp.float32)
    p2c = jnp.einsum("qhjb,jib->qhij", back, onehot, precision=lax.Precision.HIGHEST)
    logits = (content + c2p + p2c) * scale
    probs = jax.nn.softmax(logits, axis=-1).astype(jnp.bfloat16)
    context_rows = jnp.einsum("qhij,qjhd->qihd", probs, vx, preferred_element_type=jnp.float32)
    context_rows = context_rows.astype(jnp.bfloat16).reshape(group * qlen, cols)
    attn_terms = jnp.dot(context_rows, wo, preferred_element_type=jnp.float32)
    attn = sum_to_owner(attn_terms, n_mp)
    own = hidden.reshape(qry_dev * qlen, width).astype(jnp.float32)
    mid = layer_norm(own + attn).astype(jnp.bfloat16)
    chosen, lens, mid = lax.optimization_barrier((chosen, lens, mid))
    both = jnp.concatenate([mid.reshape(-1), g_proj.reshape(-1)])
    both_all = lax.all_gather(both, MP, axis=0, tiled=False)
    mid_all = both_all[:, : mid.size].reshape((n_mp * mid.shape[0], mid.shape[1]))
    proj_all = both_all[:, mid.size :].reshape((n_mp,) + g_proj.shape)
    wp = jnp.transpose(proj_all, (1, 0, 2, 3)).reshape(page_owners * n_mp * w_proj.shape[0], w_proj.shape[1])
    up = add_rows(mid_all, wu)
    inner = jax.nn.gelu(up, approximate=False).astype(jnp.bfloat16)
    down_terms = jnp.dot(inner, wd, preferred_element_type=jnp.float32)
    mlp = sum_to_owner(down_terms, n_mp)
    state = layer_norm(mid.astype(jnp.float32) + mlp).astype(jnp.bfloat16)
    width_out = w_proj.shape[1]
    proj = add_rows(state, wp)
    vectors = (proj / jnp.sqrt(jnp.sum(proj * proj, axis=-1, keepdims=True) + 1e-06)).astype(
        jnp.bfloat16
    )
    vectors = vectors.reshape(qry_dev, qlen, width_out)

    sent = jnp.broadcast_to(vectors[None], (page_owners, qry_dev, qlen, width_out))
    recv = lax.all_to_all(sent, DP, split_axis=0, concat_axis=0, tiled=True)
    rows_in = jnp.take_along_axis(recv, which_query[:, :, None, None], axis=1)
    token_positions = jnp.arange(ptok, dtype=jnp.int32)
    sim = jnp.einsum("snie,snte->snit", rows_in, chosen, preferred_element_type=jnp.float32)
    valid = token_positions[None, None, None, :] < lens[:, :, None, None]
    returned = return_maxima(jnp.max(jnp.where(valid, sim, -1e30), axis=-1))
    best = returned.reshape(page_owners * cap, qlen)[index]
    best = best.reshape(qry_dev, ncand, ppc, qlen)
    scores = jnp.sum(jnp.max(best, axis=2), axis=-1)
    return (vectors, scores)


def solution(mesh):
    in_specs = (
        P(DP + MP, None, None),
        P(DP, MP),
        P(DP, MP),
        P(DP, MP),
        P(DP, None),
        P(),
        P(MP, DP),
        P(DP, MP),
        P(MP, DP),
        P(DP + MP, None),
        P(DP, None, None),
        P(DP),
        P(),
        P(DP + MP, None, None),
    )
    out_specs = (P(DP + MP, None, None), P(DP + MP, None))
    fine = Mesh(mesh.devices.reshape(mesh.devices.shape[0] // 8, 8, mesh.devices.shape[1] // 2, 2), DP + MP)
    return jax.shard_map(body, mesh=fine, in_specs=in_specs, out_specs=out_specs, check_vma=False)
```

```python
import jax
import jax.numpy as jnp
from jax import lax
from jax.sharding import Mesh, PartitionSpec as P

HD = 64
DP = ("y", "z")
MP = ("x", "c")


def layer_norm(value):
    mean = jnp.mean(value, axis=-1, keepdims=True)
    centered = value - mean
    var = jnp.mean(centered * centered, axis=-1, keepdims=True)
    return centered / jnp.sqrt(var + 1e-07)


def add_rows(left, piece):
    return jnp.dot(left, piece, preferred_element_type=jnp.float32)


def sum_to_owner(terms, n_mp):
    pieces = terms.astype(jnp.bfloat16).reshape((n_mp, terms.shape[0] // n_mp) + terms.shape[1:])
    got = lax.all_to_all(pieces, MP, split_axis=0, concat_axis=0, tiled=True)
    return jnp.sum(got.astype(jnp.float32), axis=0).astype(jnp.bfloat16).astype(jnp.float32)


def gather_over_y(pieces, lanes):
    flat_pieces = jnp.concatenate([p.reshape(-1, lanes) for p in pieces], axis=0)
    return lax.all_gather(flat_pieces, DP[0], axis=0, tiled=False)


def gather_over_z(pieces, lanes, by_y, page_owners):
    by_zy = lax.all_gather(by_y, DP[1], axis=0, tiled=False)
    gathered = jnp.swapaxes(by_zy, 0, 1).reshape((page_owners,) + by_y.shape[1:])
    parts = []
    start = 0
    for p in pieces:
        n = p.size // lanes
        parts.append(gathered[:, start : start + n])
        start += n
    return parts


def return_maxima(maxima):
    return lax.all_to_all(
        maxima.astype(jnp.bfloat16), DP, split_axis=0, concat_axis=0, tiled=True
    ).astype(maxima.dtype)


def body(
    hidden,
    query_weight,
    w_key,
    w_value,
    rel_table,
    rel_bucket,
    w_out,
    w_up,
    w_down,
    w_proj,
    pages,
    page_len,
    slot_per_page,
    candidates,
):
    qry_dev, qlen, width = hidden.shape
    heads_local = query_weight.shape[1] // HD
    cols = query_weight.shape[1]
    page_owners = lax.axis_size(DP)
    n_mp = lax.axis_size(MP)

    pg_dev = pages.shape[0]
    ptok = pages.shape[1]
    ncand, ppc = (candidates.shape[1], candidates.shape[2])
    req = qry_dev * ncand * ppc
    cap = 2 * req // page_owners
    slots = slot_per_page[candidates.reshape(req)]
    dest = slots // pg_dev
    local = slots % pg_dev
    query_of = jnp.arange(req, dtype=jnp.int32) // (ncand * ppc)
    member = (dest[:, None] == jnp.arange(page_owners, dtype=jnp.int32)[None, :]).astype(jnp.int32)
    place = jnp.sum((jnp.cumsum(member, axis=0) - 1) * member, axis=1)
    index = dest * cap + place
    table_local = jnp.zeros((page_owners * cap,), jnp.int32).at[index].set(local)
    table_query = jnp.zeros((page_owners * cap,), jnp.int32).at[index].set(query_of)
    table = jnp.concatenate([table_local, table_query]).astype(jnp.bfloat16)

    lanes = query_weight.shape[1]
    first = (query_weight, w_key, w_value, w_out.T, rel_table, w_proj, table)
    second = (w_up, w_down.T)
    first_y = gather_over_y(first, lanes)
    first_parts = gather_over_z(first, lanes, first_y, page_owners)
    second_y = gather_over_y(second, lanes)
    first_parts, second_y = lax.optimization_barrier((first_parts, second_y))
    g_q, g_k, g_v, g_out, g_rel, g_proj, g_table = first_parts
    g_up, g_down = gather_over_z(second, lanes, second_y, page_owners)
    me = lax.axis_index(DP)
    g_table = g_table.reshape(page_owners, 2, page_owners, cap)
    mine = lax.dynamic_index_in_dim(g_table, me, axis=2, keepdims=False).astype(jnp.int32)
    where_local = mine[:, 0]
    which_query = mine[:, 1]
    chosen = pages[where_local]
    lens = page_len[where_local]
    wq = g_q.reshape(page_owners * query_weight.shape[0], cols)
    wk = g_k.reshape(page_owners * w_key.shape[0], cols)
    wv = g_v.reshape(page_owners * w_value.shape[0], cols)
    wo = g_out.reshape(page_owners * w_out.shape[1], w_out.shape[0]).T
    wu = g_up.reshape(page_owners * w_up.shape[0], w_up.shape[1])
    wd = g_down.reshape(page_owners * w_down.shape[1], w_down.shape[0]).T
    left_rel = g_rel.reshape(page_owners * rel_table.shape[0], rel_table.shape[1])
    g_proj = g_proj.reshape((page_owners,) + w_proj.shape)

    spread = jnp.broadcast_to(hidden[None], (n_mp,) + hidden.shape)
    tokens = lax.all_to_all(spread, MP, split_axis=0, concat_axis=0, tiled=True)
    tokens = tokens.reshape((n_mp * qry_dev,) + hidden.shape[1:])
    group = tokens.shape[0]
    flat = tokens.reshape(group * qlen, width)
    qsum = add_rows(flat, wq)
    ksum = add_rows(flat, wk)
    vsum = add_rows(flat, wv)
    qrsum = add_rows(left_rel, wq)
    krsum = add_rows(left_rel, wk)
    rel_q = qrsum.astype(jnp.bfloat16)
    rel_k = krsum.astype(jnp.bfloat16)
    nbuck = rel_q.shape[0]
    qx = qsum.astype(jnp.bfloat16).reshape(group, qlen, heads_local, HD)
    kx = ksum.astype(jnp.bfloat16).reshape(group, qlen, heads_local, HD)
    vx = vsum.astype(jnp.bfloat16).reshape(group, qlen, heads_local, HD)
    rel_q = rel_q.reshape(nbuck, heads_local, HD)
    rel_k = rel_k.reshape(nbuck, heads_local, HD)
    onehot = (rel_bucket[:, :, None] == jnp.arange(nbuck, dtype=jnp.int32)[None, None, :]).astype(
        jnp.float32
    )
    scale = 1.0 / jnp.sqrt(jnp.float32(3 * HD))
    content = jnp.einsum("qihd,qjhd->qhij", qx, kx, preferred_element_type=jnp.float32)
    along_axis_name = jnp.einsum("qihd,bhd->qhib", qx, rel_k, preferred_element_type=jnp.float32)
    c2p = jnp.einsum("qhib,ijb->qhij", along_axis_name, onehot, precision=lax.Precision.HIGHEST)
    back = jnp.einsum("qjhd,bhd->qhjb", kx, rel_q, preferred_element_type=jnp.float32)
    p2c = jnp.einsum("qhjb,jib->qhij", back, onehot, precision=lax.Precision.HIGHEST)
    logits = (content + c2p + p2c) * scale
    probs = jax.nn.softmax(logits, axis=-1).astype(jnp.bfloat16)
    context_rows = jnp.einsum("qhij,qjhd->qihd", probs, vx, preferred_element_type=jnp.float32)
    context_rows = context_rows.astype(jnp.bfloat16).reshape(group * qlen, cols)
    attn_terms = jnp.dot(context_rows, wo, preferred_element_type=jnp.float32)
    attn = sum_to_owner(attn_terms, n_mp)
    own = hidden.reshape(qry_dev * qlen, width).astype(jnp.float32)
    mid = layer_norm(own + attn).astype(jnp.bfloat16)
    both = jnp.concatenate([mid, g_proj.reshape(-1, mid.shape[1])], axis=0)
    both_all = lax.all_to_all(
        jnp.broadcast_to(both[None], (n_mp,) + both.shape), MP, split_axis=0, concat_axis=0, tiled=True
    )
    mid_all = both_all[:, : mid.shape[0]].reshape((n_mp * mid.shape[0], mid.shape[1]))
    proj_all = both_all[:, mid.shape[0] :].reshape((n_mp,) + g_proj.shape)
    wp = jnp.transpose(proj_all, (1, 0, 2, 3)).reshape(page_owners * n_mp * w_proj.shape[0], w_proj.shape[1])
    chosen, lens, mid_all = lax.optimization_barrier((chosen, lens, mid_all))
    up = add_rows(mid_all, wu)
    inner = jax.nn.gelu(up, approximate=False).astype(jnp.bfloat16)
    down_terms = jnp.dot(inner, wd, preferred_element_type=jnp.float32)
    mlp = sum_to_owner(down_terms, n_mp)
    state = layer_norm(mid.astype(jnp.float32) + mlp).astype(jnp.bfloat16)
    width_out = w_proj.shape[1]
    proj = add_rows(state, wp)
    vectors = (proj / jnp.sqrt(jnp.sum(proj * proj, axis=-1, keepdims=True) + 1e-06)).astype(
        jnp.bfloat16
    )
    vectors = vectors.reshape(qry_dev, qlen, width_out)

    sent = jnp.broadcast_to(vectors[None], (page_owners, qry_dev, qlen, width_out))
    recv = lax.all_to_all(sent, DP, split_axis=0, concat_axis=0, tiled=True)
    rows_in = jnp.take_along_axis(recv, which_query[:, :, None, None], axis=1)
    token_positions = jnp.arange(ptok, dtype=jnp.int32)
    sim = jnp.einsum("snie,snte->snit", rows_in, chosen, preferred_element_type=jnp.float32)
    valid = token_positions[None, None, None, :] < lens[:, :, None, None]
    returned = return_maxima(jnp.max(jnp.where(valid, sim, -1e30), axis=-1))
    best = returned.reshape(page_owners * cap, qlen)[index]
    best = best.reshape(qry_dev, ncand, ppc, qlen)
    scores = jnp.sum(jnp.max(best, axis=2), axis=-1)
    return (vectors, scores)


def solution(mesh):
    in_specs = (
        P(DP + MP, None, None),
        P(DP, MP),
        P(DP, MP),
        P(DP, MP),
        P(DP, None),
        P(),
        P(MP, DP),
        P(DP, MP),
        P(MP, DP),
        P(DP + MP, None),
        P(DP, None, None),
        P(DP),
        P(),
        P(DP + MP, None, None),
    )
    out_specs = (P(DP + MP, None, None), P(DP + MP, None))
    fine = Mesh(mesh.devices.reshape(mesh.devices.shape[0] // 8, 8, mesh.devices.shape[1] // 2, 2), DP + MP)
    return jax.shard_map(body, mesh=fine, in_specs=in_specs, out_specs=out_specs, check_vma=False)
```

```python
from functools import partial

import jax
import jax.numpy as jnp
from jax import lax
from jax.sharding import Mesh, PartitionSpec as P

HD = 64
DP = ("y", "z")
MP = ("x", "c")


def layer_norm(value):
    mean = jnp.mean(value, axis=-1, keepdims=True)
    centered = value - mean
    var = jnp.mean(centered * centered, axis=-1, keepdims=True)
    return centered / jnp.sqrt(var + 1e-07)


def add_rows(left, piece):
    return jnp.dot(left, piece, preferred_element_type=jnp.float32)


def sum_to_owner(terms, n_mp):
    pieces = terms.astype(jnp.bfloat16).reshape((n_mp, terms.shape[0] // n_mp) + terms.shape[1:])
    got = lax.all_to_all(pieces, MP, split_axis=0, concat_axis=0, tiled=True)
    return jnp.sum(got.astype(jnp.float32), axis=0).astype(jnp.bfloat16).astype(jnp.float32)


def ring_gather(x, axis_name, size):
    by_offset = [None] * size
    by_offset[0] = x
    fwd = x
    bwd = x
    for step in range(1, size // 2 + 1):
        fwd = lax.ppermute(fwd, axis_name, [(i, (i + 1) % size) for i in range(size)])
        by_offset[size - step] = fwd
        if step < size - step:
            bwd = lax.ppermute(bwd, axis_name, [(i, (i - 1) % size) for i in range(size)])
            by_offset[step] = bwd
    stacked = jnp.stack(by_offset)
    me = lax.axis_index(axis_name)
    return jnp.take(stacked, (jnp.arange(size, dtype=jnp.int32) - me) % size, axis=0)


def gather_rows(pieces, lanes, page_owners, sizes):
    flat_pieces = jnp.concatenate([p.reshape(-1, lanes) for p in pieces], axis=0)
    by_z = ring_gather(flat_pieces, DP[1], sizes[DP[1]])
    by_yz = ring_gather(by_z, DP[0], sizes[DP[0]])
    gathered = by_yz.reshape((page_owners,) + flat_pieces.shape)
    parts = []
    start = 0
    for p in pieces:
        n = p.size // lanes
        parts.append(gathered[:, start : start + n])
        start += n
    return parts


def return_maxima(maxima):
    return lax.all_to_all(
        maxima.astype(jnp.bfloat16), DP, split_axis=0, concat_axis=0, tiled=True
    ).astype(maxima.dtype)


def body(
    sizes,
    hidden,
    query_weight,
    w_key,
    w_value,
    rel_table,
    rel_bucket,
    w_out,
    w_up,
    w_down,
    w_proj,
    pages,
    page_len,
    slot_per_page,
    candidates,
):
    qry_dev, qlen, width = hidden.shape
    heads_local = query_weight.shape[1] // HD
    cols = query_weight.shape[1]
    page_owners = lax.axis_size(DP)
    n_mp = lax.axis_size(MP)

    pg_dev = pages.shape[0]
    ptok = pages.shape[1]
    ncand, ppc = (candidates.shape[1], candidates.shape[2])
    req = qry_dev * ncand * ppc
    cap = 2 * req // page_owners
    slots = slot_per_page[candidates.reshape(req)]
    dest = slots // pg_dev
    local = slots % pg_dev
    query_of = jnp.arange(req, dtype=jnp.int32) // (ncand * ppc)
    member = (dest[:, None] == jnp.arange(page_owners, dtype=jnp.int32)[None, :]).astype(jnp.int32)
    place = jnp.sum((jnp.cumsum(member, axis=0) - 1) * member, axis=1)
    index = dest * cap + place
    table_local = jnp.zeros((page_owners * cap,), jnp.int32).at[index].set(local)
    table_query = jnp.zeros((page_owners * cap,), jnp.int32).at[index].set(query_of)
    table = jnp.concatenate([table_local, table_query]).astype(jnp.bfloat16)

    lanes = query_weight.shape[1]
    first = (query_weight, w_key, w_value, w_out.T, rel_table, w_proj, table)
    second = (w_up, w_down.T)
    g_q, g_k, g_v, g_out, g_rel, g_proj, g_table = gather_rows(first, lanes, page_owners, sizes)
    g_up, g_down = gather_rows(second, lanes, page_owners, sizes)
    me = lax.axis_index(DP)
    g_table = g_table.reshape(page_owners, 2, page_owners, cap)
    mine = lax.dynamic_index_in_dim(g_table, me, axis=2, keepdims=False).astype(jnp.int32)
    where_local = mine[:, 0]
    which_query = mine[:, 1]
    chosen = pages[where_local]
    lens = page_len[where_local]
    wq = g_q.reshape(page_owners * query_weight.shape[0], cols)
    wk = g_k.reshape(page_owners * w_key.shape[0], cols)
    wv = g_v.reshape(page_owners * w_value.shape[0], cols)
    wo = g_out.reshape(page_owners * w_out.shape[1], w_out.shape[0]).T
    wu = g_up.reshape(page_owners * w_up.shape[0], w_up.shape[1])
    wd = g_down.reshape(page_owners * w_down.shape[1], w_down.shape[0]).T
    left_rel = g_rel.reshape(page_owners * rel_table.shape[0], rel_table.shape[1])
    g_proj = g_proj.reshape((page_owners,) + w_proj.shape)

    spread = jnp.broadcast_to(hidden[None], (n_mp,) + hidden.shape)
    tokens = lax.all_to_all(spread, MP, split_axis=0, concat_axis=0, tiled=True)
    tokens = tokens.reshape((n_mp * qry_dev,) + hidden.shape[1:])
    group = tokens.shape[0]
    flat = tokens.reshape(group * qlen, width)
    qsum = add_rows(flat, wq)
    ksum = add_rows(flat, wk)
    vsum = add_rows(flat, wv)
    qrsum = add_rows(left_rel, wq)
    krsum = add_rows(left_rel, wk)
    rel_q = qrsum.astype(jnp.bfloat16)
    rel_k = krsum.astype(jnp.bfloat16)
    nbuck = rel_q.shape[0]
    qx = qsum.astype(jnp.bfloat16).reshape(group, qlen, heads_local, HD)
    kx = ksum.astype(jnp.bfloat16).reshape(group, qlen, heads_local, HD)
    vx = vsum.astype(jnp.bfloat16).reshape(group, qlen, heads_local, HD)
    rel_q = rel_q.reshape(nbuck, heads_local, HD)
    rel_k = rel_k.reshape(nbuck, heads_local, HD)
    onehot = (rel_bucket[:, :, None] == jnp.arange(nbuck, dtype=jnp.int32)[None, None, :]).astype(
        jnp.float32
    )
    scale = 1.0 / jnp.sqrt(jnp.float32(3 * HD))
    content = jnp.einsum("qihd,qjhd->qhij", qx, kx, preferred_element_type=jnp.float32)
    along_axis_name = jnp.einsum("qihd,bhd->qhib", qx, rel_k, preferred_element_type=jnp.float32)
    c2p = jnp.einsum("qhib,ijb->qhij", along_axis_name, onehot, precision=lax.Precision.HIGHEST)
    back = jnp.einsum("qjhd,bhd->qhjb", kx, rel_q, preferred_element_type=jnp.float32)
    p2c = jnp.einsum("qhjb,jib->qhij", back, onehot, precision=lax.Precision.HIGHEST)
    logits = (content + c2p + p2c) * scale
    probs = jax.nn.softmax(logits, axis=-1).astype(jnp.bfloat16)
    context_rows = jnp.einsum("qhij,qjhd->qihd", probs, vx, preferred_element_type=jnp.float32)
    context_rows = context_rows.astype(jnp.bfloat16).reshape(group * qlen, cols)
    attn_terms = jnp.dot(context_rows, wo, preferred_element_type=jnp.float32)
    attn = sum_to_owner(attn_terms, n_mp)
    own = hidden.reshape(qry_dev * qlen, width).astype(jnp.float32)
    mid = layer_norm(own + attn).astype(jnp.bfloat16)
    both = jnp.concatenate([mid, g_proj.reshape(-1, mid.shape[1])], axis=0)
    both_all = lax.all_to_all(
        jnp.broadcast_to(both[None], (n_mp,) + both.shape), MP, split_axis=0, concat_axis=0, tiled=True
    )
    mid_all = both_all[:, : mid.shape[0]].reshape((n_mp * mid.shape[0], mid.shape[1]))
    proj_all = both_all[:, mid.shape[0] :].reshape((n_mp,) + g_proj.shape)
    wp = jnp.transpose(proj_all, (1, 0, 2, 3)).reshape(page_owners * n_mp * w_proj.shape[0], w_proj.shape[1])
    chosen, lens, mid_all = lax.optimization_barrier((chosen, lens, mid_all))
    up = add_rows(mid_all, wu)
    inner = jax.nn.gelu(up, approximate=False).astype(jnp.bfloat16)
    down_terms = jnp.dot(inner, wd, preferred_element_type=jnp.float32)
    mlp = sum_to_owner(down_terms, n_mp)
    state = layer_norm(mid.astype(jnp.float32) + mlp).astype(jnp.bfloat16)
    width_out = w_proj.shape[1]
    proj = add_rows(state, wp)
    vectors = (proj / jnp.sqrt(jnp.sum(proj * proj, axis=-1, keepdims=True) + 1e-06)).astype(
        jnp.bfloat16
    )
    vectors = vectors.reshape(qry_dev, qlen, width_out)

    sent = jnp.broadcast_to(vectors[None], (page_owners, qry_dev, qlen, width_out))
    recv = lax.all_to_all(sent, DP, split_axis=0, concat_axis=0, tiled=True)
    rows_in = jnp.take_along_axis(recv, which_query[:, :, None, None], axis=1)
    token_positions = jnp.arange(ptok, dtype=jnp.int32)
    sim = jnp.einsum("snie,snte->snit", rows_in, chosen, preferred_element_type=jnp.float32)
    valid = token_positions[None, None, None, :] < lens[:, :, None, None]
    returned = return_maxima(jnp.max(jnp.where(valid, sim, -1e30), axis=-1))
    best = returned.reshape(page_owners * cap, qlen)[index]
    best = best.reshape(qry_dev, ncand, ppc, qlen)
    scores = jnp.sum(jnp.max(best, axis=2), axis=-1)
    return (vectors, scores)


def solution(mesh):
    in_specs = (
        P(DP + MP, None, None),
        P(DP, MP),
        P(DP, MP),
        P(DP, MP),
        P(DP, None),
        P(),
        P(MP, DP),
        P(DP, MP),
        P(MP, DP),
        P(DP + MP, None),
        P(DP, None, None),
        P(DP),
        P(),
        P(DP + MP, None, None),
    )
    out_specs = (P(DP + MP, None, None), P(DP + MP, None))
    fine = Mesh(mesh.devices.reshape(mesh.devices.shape[0] // 8, 8, mesh.devices.shape[1] // 2, 2), DP + MP)
    sizes = dict(zip(fine.axis_names, fine.devices.shape))
    return jax.shard_map(partial(body, sizes), mesh=fine, in_specs=in_specs, out_specs=out_specs, check_vma=False)
```

```python
import jax
import jax.numpy as jnp
from jax import lax
from jax.sharding import Mesh, PartitionSpec as P

HD = 64
DP = ("y", "z")
MP = ("x", "c")


def layer_norm(value):
    mean = jnp.mean(value, axis=-1, keepdims=True)
    centered = value - mean
    var = jnp.mean(centered * centered, axis=-1, keepdims=True)
    return centered / jnp.sqrt(var + 1e-07)


def add_rows(left, piece):
    return jnp.dot(left, piece, preferred_element_type=jnp.float32)


def sum_to_owner(terms, n_mp):
    pieces = terms.astype(jnp.bfloat16).reshape((n_mp, terms.shape[0] // n_mp) + terms.shape[1:])
    got = lax.all_to_all(pieces, MP, split_axis=0, concat_axis=0, tiled=True)
    return jnp.sum(got.astype(jnp.float32), axis=0).astype(jnp.bfloat16).astype(jnp.float32)


def gather_over_y(pieces, lanes):
    flat_pieces = jnp.concatenate([p.reshape(-1, lanes) for p in pieces], axis=0)
    return lax.all_gather(flat_pieces, DP[0], axis=0, tiled=False)


def gather_over_z(pieces, lanes, by_y, page_owners):
    by_yz = lax.all_gather(by_y, DP[1], axis=1, tiled=False)
    gathered = by_yz.reshape((page_owners,) + by_y.shape[1:])
    parts = []
    start = 0
    for p in pieces:
        n = p.size // lanes
        parts.append(gathered[:, start : start + n])
        start += n
    return parts


def return_maxima(maxima):
    return lax.all_to_all(
        maxima.astype(jnp.bfloat16), DP, split_axis=0, concat_axis=0, tiled=True
    ).astype(maxima.dtype)


def body(
    hidden,
    query_weight,
    w_key,
    w_value,
    rel_table,
    rel_bucket,
    w_out,
    w_up,
    w_down,
    w_proj,
    pages,
    page_len,
    slot_per_page,
    candidates,
):
    qry_dev, qlen, width = hidden.shape
    heads_local = query_weight.shape[1] // HD
    cols = query_weight.shape[1]
    page_owners = lax.axis_size(DP)
    n_mp = lax.axis_size(MP)

    lanes = query_weight.shape[1]
    first = (query_weight, w_key, w_value, w_out.T, rel_table, w_proj)
    second = (w_up, w_down.T)
    first_y = gather_over_y(first, lanes)
    first_parts = gather_over_z(first, lanes, first_y, page_owners)
    pg_dev = pages.shape[0]
    ptok = pages.shape[1]
    ncand, ppc = (candidates.shape[1], candidates.shape[2])
    req = qry_dev * ncand * ppc
    cap = 2 * req // page_owners
    first_y, candidates = lax.optimization_barrier((first_y, candidates))
    slots = slot_per_page[candidates.reshape(req)]
    dest = slots // pg_dev
    local = slots % pg_dev
    query_of = jnp.arange(req, dtype=jnp.int32) // (ncand * ppc)
    member = (dest[:, None] == jnp.arange(page_owners, dtype=jnp.int32)[None, :]).astype(jnp.int32)
    place = jnp.sum((jnp.cumsum(member, axis=0) - 1) * member, axis=1)
    index = dest * cap + place
    codes = jnp.zeros((page_owners * cap,), jnp.int32).at[index].set(query_of * pg_dev + local)
    got = lax.all_to_all(codes.reshape(page_owners, cap), DP, split_axis=0, concat_axis=0, tiled=True)
    second_y = gather_over_y(second, lanes)
    first_parts, second_y, got = lax.optimization_barrier((first_parts, second_y, got))
    where_local = got % pg_dev
    which_query = got // pg_dev

    g_q, g_k, g_v, g_out, g_rel, g_proj = first_parts
    g_up, g_down = gather_over_z(second, lanes, second_y, page_owners)
    chosen = pages[where_local]
    lens = page_len[where_local]
    wq = g_q.reshape(page_owners * query_weight.shape[0], cols)
    wk = g_k.reshape(page_owners * w_key.shape[0], cols)
    wv = g_v.reshape(page_owners * w_value.shape[0], cols)
    wo = g_out.reshape(page_owners * w_out.shape[1], w_out.shape[0]).T
    wu = g_up.reshape(page_owners * w_up.shape[0], w_up.shape[1])
    wd = g_down.reshape(page_owners * w_down.shape[1], w_down.shape[0]).T
    left_rel = g_rel.reshape(page_owners * rel_table.shape[0], rel_table.shape[1])
    g_proj = g_proj.reshape((page_owners,) + w_proj.shape)

    spread = jnp.broadcast_to(hidden[None], (n_mp,) + hidden.shape)
    tokens = lax.all_to_all(spread, MP, split_axis=0, concat_axis=0, tiled=True)
    tokens = tokens.reshape((n_mp * qry_dev,) + hidden.shape[1:])
    group = tokens.shape[0]
    flat = tokens.reshape(group * qlen, width)
    qsum = add_rows(flat, wq)
    ksum = add_rows(flat, wk)
    vsum = add_rows(flat, wv)
    qrsum = add_rows(left_rel, wq)
    krsum = add_rows(left_rel, wk)
    rel_q = qrsum.astype(jnp.bfloat16)
    rel_k = krsum.astype(jnp.bfloat16)
    nbuck = rel_q.shape[0]
    qx = qsum.astype(jnp.bfloat16).reshape(group, qlen, heads_local, HD)
    kx = ksum.astype(jnp.bfloat16).reshape(group, qlen, heads_local, HD)
    vx = vsum.astype(jnp.bfloat16).reshape(group, qlen, heads_local, HD)
    rel_q = rel_q.reshape(nbuck, heads_local, HD)
    rel_k = rel_k.reshape(nbuck, heads_local, HD)
    onehot = (rel_bucket[:, :, None] == jnp.arange(nbuck, dtype=jnp.int32)[None, None, :]).astype(
        jnp.float32
    )
    scale = 1.0 / jnp.sqrt(jnp.float32(3 * HD))
    content = jnp.einsum("qihd,qjhd->qhij", qx, kx, preferred_element_type=jnp.float32)
    along_axis_name = jnp.einsum("qihd,bhd->qhib", qx, rel_k, preferred_element_type=jnp.float32)
    c2p = jnp.einsum("qhib,ijb->qhij", along_axis_name, onehot, precision=lax.Precision.HIGHEST)
    back = jnp.einsum("qjhd,bhd->qhjb", kx, rel_q, preferred_element_type=jnp.float32)
    p2c = jnp.einsum("qhjb,jib->qhij", back, onehot, precision=lax.Precision.HIGHEST)
    logits = (content + c2p + p2c) * scale
    probs = jax.nn.softmax(logits, axis=-1).astype(jnp.bfloat16)
    context_rows = jnp.einsum("qhij,qjhd->qihd", probs, vx, preferred_element_type=jnp.float32)
    context_rows = context_rows.astype(jnp.bfloat16).reshape(group * qlen, cols)
    attn_terms = jnp.dot(context_rows, wo, preferred_element_type=jnp.float32)
    attn = sum_to_owner(attn_terms, n_mp)
    own = hidden.reshape(qry_dev * qlen, width).astype(jnp.float32)
    mid = layer_norm(own + attn).astype(jnp.bfloat16)
    both = jnp.concatenate([mid, g_proj.reshape(-1, mid.shape[1])], axis=0)
    both_all = lax.all_to_all(
        jnp.broadcast_to(both[None], (n_mp,) + both.shape), MP, split_axis=0, concat_axis=0, tiled=True
    )
    mid_all = both_all[:, : mid.shape[0]].reshape((n_mp * mid.shape[0], mid.shape[1]))
    proj_all = both_all[:, mid.shape[0] :].reshape((n_mp,) + g_proj.shape)
    wp = jnp.transpose(proj_all, (1, 0, 2, 3)).reshape(page_owners * n_mp * w_proj.shape[0], w_proj.shape[1])
    chosen, lens, mid_all = lax.optimization_barrier((chosen, lens, mid_all))
    up = add_rows(mid_all, wu)
    inner = jax.nn.gelu(up, approximate=False).astype(jnp.bfloat16)
    down_terms = jnp.dot(inner, wd, preferred_element_type=jnp.float32)
    mlp = sum_to_owner(down_terms, n_mp)
    state = layer_norm(mid.astype(jnp.float32) + mlp).astype(jnp.bfloat16)
    width_out = w_proj.shape[1]
    proj = add_rows(state, wp)
    vectors = (proj / jnp.sqrt(jnp.sum(proj * proj, axis=-1, keepdims=True) + 1e-06)).astype(
        jnp.bfloat16
    )
    vectors = vectors.reshape(qry_dev, qlen, width_out)

    sent = jnp.broadcast_to(vectors[None], (page_owners, qry_dev, qlen, width_out))
    recv = lax.all_to_all(sent, DP, split_axis=0, concat_axis=0, tiled=True)
    rows_in = jnp.take_along_axis(recv, which_query[:, :, None, None], axis=1)
    token_positions = jnp.arange(ptok, dtype=jnp.int32)
    sim = jnp.einsum("snie,snte->snit", rows_in, chosen, preferred_element_type=jnp.float32)
    valid = token_positions[None, None, None, :] < lens[:, :, None, None]
    returned = return_maxima(jnp.max(jnp.where(valid, sim, -1e30), axis=-1))
    best = returned.reshape(page_owners * cap, qlen)[index]
    best = best.reshape(qry_dev, ncand, ppc, qlen)
    scores = jnp.sum(jnp.max(best, axis=2), axis=-1)
    return (vectors, scores)


def solution(mesh):
    in_specs = (
        P(DP + MP, None, None),
        P(DP, MP),
        P(DP, MP),
        P(DP, MP),
        P(DP, None),
        P(),
        P(MP, DP),
        P(DP, MP),
        P(MP, DP),
        P(DP + MP, None),
        P(DP, None, None),
        P(DP),
        P(),
        P(DP + MP, None, None),
    )
    out_specs = (P(DP + MP, None, None), P(DP + MP, None))
    fine = Mesh(mesh.devices.reshape(mesh.devices.shape[0] // 8, 8, mesh.devices.shape[1] // 2, 2), DP + MP)
    return jax.shard_map(body, mesh=fine, in_specs=in_specs, out_specs=out_specs, check_vma=False)
```

```python
import jax
import jax.numpy as jnp
from jax import lax
from jax.sharding import Mesh, PartitionSpec as P

HD = 64
DP = ("y", "z")
MP = ("x", "c")


def layer_norm(value):
    mean = jnp.mean(value, axis=-1, keepdims=True)
    centered = value - mean
    var = jnp.mean(centered * centered, axis=-1, keepdims=True)
    return centered / jnp.sqrt(var + 1e-07)


def add_rows(left, piece):
    return jnp.dot(left, piece, preferred_element_type=jnp.float32)


def sum_to_owner(terms, n_mp):
    pieces = terms.astype(jnp.bfloat16).reshape((n_mp, terms.shape[0] // n_mp) + terms.shape[1:])
    got = lax.all_to_all(pieces, MP, split_axis=0, concat_axis=0, tiled=True)
    return jnp.sum(got.astype(jnp.float32), axis=0).astype(jnp.bfloat16).astype(jnp.float32)


def gather_over_y(pieces, lanes):
    rows = sum(p.size // lanes for p in pieces)
    pad = jnp.zeros((-rows % 16, lanes), pieces[0].dtype)
    flat_pieces = jnp.concatenate([p.reshape(-1, lanes) for p in pieces] + [pad], axis=0)
    return lax.all_gather(flat_pieces, DP[0], axis=0, tiled=False)


def gather_over_z(pieces, lanes, by_y, page_owners):
    by_yz = lax.all_gather(by_y, DP[1], axis=1, tiled=False)
    gathered = by_yz.reshape((page_owners,) + by_y.shape[1:])
    parts = []
    start = 0
    for p in pieces:
        n = p.size // lanes
        parts.append(gathered[:, start : start + n])
        start += n
    return parts


def return_maxima(maxima):
    return lax.all_to_all(
        maxima.astype(jnp.bfloat16), DP, split_axis=0, concat_axis=0, tiled=True
    ).astype(maxima.dtype)


def body(
    hidden,
    query_weight,
    w_key,
    w_value,
    rel_table,
    rel_bucket,
    w_out,
    w_up,
    w_down,
    w_proj,
    pages,
    page_len,
    slot_per_page,
    candidates,
):
    qry_dev, qlen, width = hidden.shape
    heads_local = query_weight.shape[1] // HD
    cols = query_weight.shape[1]
    page_owners = lax.axis_size(DP)
    n_mp = lax.axis_size(MP)

    lanes = query_weight.shape[1]
    first = (query_weight, w_key, w_value, w_out.T, rel_table, w_proj)
    second = (w_up, w_down.T)
    first_y = gather_over_y(first, lanes)
    first_parts = gather_over_z(first, lanes, first_y, page_owners)
    pg_dev = pages.shape[0]
    ptok = pages.shape[1]
    ncand, ppc = (candidates.shape[1], candidates.shape[2])
    req = qry_dev * ncand * ppc
    cap = 2 * req // page_owners
    first_y, candidates = lax.optimization_barrier((first_y, candidates))
    slots = slot_per_page[candidates.reshape(req)]
    dest = slots // pg_dev
    local = slots % pg_dev
    query_of = jnp.arange(req, dtype=jnp.int32) // (ncand * ppc)
    member = (dest[:, None] == jnp.arange(page_owners, dtype=jnp.int32)[None, :]).astype(jnp.int32)
    place = jnp.sum((jnp.cumsum(member, axis=0) - 1) * member, axis=1)
    index = dest * cap + place
    codes = jnp.zeros((page_owners * cap,), jnp.int32).at[index].set(query_of * pg_dev + local)
    got = lax.all_to_all(codes.reshape(page_owners, cap), DP, split_axis=0, concat_axis=0, tiled=True)
    second_y = gather_over_y(second, lanes)
    first_parts, second_y, got = lax.optimization_barrier((first_parts, second_y, got))
    where_local = got % pg_dev
    which_query = got // pg_dev

    g_q, g_k, g_v, g_out, g_rel, g_proj = first_parts
    g_up, g_down = gather_over_z(second, lanes, second_y, page_owners)
    chosen = pages[where_local]
    lens = page_len[where_local]
    wq = g_q.reshape(page_owners * query_weight.shape[0], cols)
    wk = g_k.reshape(page_owners * w_key.shape[0], cols)
    wv = g_v.reshape(page_owners * w_value.shape[0], cols)
    wo = g_out.reshape(page_owners * w_out.shape[1], w_out.shape[0]).T
    wu = g_up.reshape(page_owners * w_up.shape[0], w_up.shape[1])
    wd = g_down.reshape(page_owners * w_down.shape[1], w_down.shape[0]).T
    left_rel = g_rel.reshape(page_owners * rel_table.shape[0], rel_table.shape[1])
    g_proj = g_proj.reshape((page_owners,) + w_proj.shape)

    spread = jnp.broadcast_to(hidden[None], (n_mp,) + hidden.shape)
    tokens = lax.all_to_all(spread, MP, split_axis=0, concat_axis=0, tiled=True)
    tokens = tokens.reshape((n_mp * qry_dev,) + hidden.shape[1:])
    group = tokens.shape[0]
    flat = tokens.reshape(group * qlen, width)
    qsum = add_rows(flat, wq)
    ksum = add_rows(flat, wk)
    vsum = add_rows(flat, wv)
    qrsum = add_rows(left_rel, wq)
    krsum = add_rows(left_rel, wk)
    rel_q = qrsum.astype(jnp.bfloat16)
    rel_k = krsum.astype(jnp.bfloat16)
    nbuck = rel_q.shape[0]
    qx = qsum.astype(jnp.bfloat16).reshape(group, qlen, heads_local, HD)
    kx = ksum.astype(jnp.bfloat16).reshape(group, qlen, heads_local, HD)
    vx = vsum.astype(jnp.bfloat16).reshape(group, qlen, heads_local, HD)
    rel_q = rel_q.reshape(nbuck, heads_local, HD)
    rel_k = rel_k.reshape(nbuck, heads_local, HD)
    onehot = (rel_bucket[:, :, None] == jnp.arange(nbuck, dtype=jnp.int32)[None, None, :]).astype(
        jnp.float32
    )
    scale = 1.0 / jnp.sqrt(jnp.float32(3 * HD))
    content = jnp.einsum("qihd,qjhd->qhij", qx, kx, preferred_element_type=jnp.float32)
    along_axis_name = jnp.einsum("qihd,bhd->qhib", qx, rel_k, preferred_element_type=jnp.float32)
    c2p = jnp.einsum("qhib,ijb->qhij", along_axis_name, onehot, precision=lax.Precision.HIGHEST)
    back = jnp.einsum("qjhd,bhd->qhjb", kx, rel_q, preferred_element_type=jnp.float32)
    p2c = jnp.einsum("qhjb,jib->qhij", back, onehot, precision=lax.Precision.HIGHEST)
    logits = (content + c2p + p2c) * scale
    probs = jax.nn.softmax(logits, axis=-1).astype(jnp.bfloat16)
    context_rows = jnp.einsum("qhij,qjhd->qihd", probs, vx, preferred_element_type=jnp.float32)
    context_rows = context_rows.astype(jnp.bfloat16).reshape(group * qlen, cols)
    attn_terms = jnp.dot(context_rows, wo, preferred_element_type=jnp.float32)
    attn = sum_to_owner(attn_terms, n_mp)
    own = hidden.reshape(qry_dev * qlen, width).astype(jnp.float32)
    mid = layer_norm(own + attn).astype(jnp.bfloat16)
    chosen, lens, mid = lax.optimization_barrier((chosen, lens, mid))
    both = jnp.concatenate([mid, g_proj.reshape(-1, mid.shape[1])], axis=0)
    both_all = lax.all_to_all(
        jnp.broadcast_to(both[None], (n_mp,) + both.shape), MP, split_axis=0, concat_axis=0, tiled=True
    )
    mid_all = both_all[:, : mid.shape[0]].reshape((n_mp * mid.shape[0], mid.shape[1]))
    proj_all = both_all[:, mid.shape[0] :].reshape((n_mp,) + g_proj.shape)
    wp = jnp.transpose(proj_all, (1, 0, 2, 3)).reshape(page_owners * n_mp * w_proj.shape[0], w_proj.shape[1])
    up = add_rows(mid_all, wu)
    inner = jax.nn.gelu(up, approximate=False).astype(jnp.bfloat16)
    down_terms = jnp.dot(inner, wd, preferred_element_type=jnp.float32)
    mlp = sum_to_owner(down_terms, n_mp)
    state = layer_norm(mid.astype(jnp.float32) + mlp).astype(jnp.bfloat16)
    width_out = w_proj.shape[1]
    proj = add_rows(state, wp)
    vectors = (proj / jnp.sqrt(jnp.sum(proj * proj, axis=-1, keepdims=True) + 1e-06)).astype(
        jnp.bfloat16
    )
    vectors = vectors.reshape(qry_dev, qlen, width_out)

    sent = jnp.broadcast_to(vectors[None], (page_owners, qry_dev, qlen, width_out))
    recv = lax.all_to_all(sent, DP, split_axis=0, concat_axis=0, tiled=True)
    rows_in = jnp.take_along_axis(recv, which_query[:, :, None, None], axis=1)
    token_positions = jnp.arange(ptok, dtype=jnp.int32)
    sim = jnp.einsum("snie,snte->snit", rows_in, chosen, preferred_element_type=jnp.float32)
    valid = token_positions[None, None, None, :] < lens[:, :, None, None]
    returned = return_maxima(jnp.max(jnp.where(valid, sim, -1e30), axis=-1))
    best = returned.reshape(page_owners * cap, qlen)[index]
    best = best.reshape(qry_dev, ncand, ppc, qlen)
    scores = jnp.sum(jnp.max(best, axis=2), axis=-1)
    return (vectors, scores)


def solution(mesh):
    in_specs = (
        P(DP + MP, None, None),
        P(DP, MP),
        P(DP, MP),
        P(DP, MP),
        P(DP, None),
        P(),
        P(MP, DP),
        P(DP, MP),
        P(MP, DP),
        P(DP + MP, None),
        P(DP, None, None),
        P(DP),
        P(),
        P(DP + MP, None, None),
    )
    out_specs = (P(DP + MP, None, None), P(DP + MP, None))
    fine = Mesh(mesh.devices.reshape(mesh.devices.shape[0] // 8, 8, mesh.devices.shape[1] // 2, 2), DP + MP)
    return jax.shard_map(body, mesh=fine, in_specs=in_specs, out_specs=out_specs, check_vma=False)
```

```python
import jax
import jax.numpy as jnp
from jax import lax
from jax.sharding import Mesh, PartitionSpec as P

HD = 64
DP = ("y", "z")
MP = ("x", "c")


def layer_norm(value):
    mean = jnp.mean(value, axis=-1, keepdims=True)
    centered = value - mean
    var = jnp.mean(centered * centered, axis=-1, keepdims=True)
    return centered / jnp.sqrt(var + 1e-07)


def add_rows(left, piece):
    return jnp.dot(left, piece, preferred_element_type=jnp.float32)


def sum_to_owner(terms, n_mp):
    pieces = terms.astype(jnp.bfloat16).reshape((n_mp, terms.shape[0] // n_mp) + terms.shape[1:])
    got = lax.all_to_all(pieces, MP, split_axis=0, concat_axis=0, tiled=True)
    return jnp.sum(got.astype(jnp.float32), axis=0).astype(jnp.bfloat16).astype(jnp.float32)


def gather_over_y(pieces, lanes):
    rows = sum(p.size // lanes for p in pieces)
    pad = jnp.zeros((-rows % 16, lanes), pieces[0].dtype)
    flat_pieces = jnp.concatenate([p.reshape(-1, lanes) for p in pieces] + [pad], axis=0)
    return lax.all_gather(flat_pieces, DP[0], axis=0, tiled=False)


def gather_over_z(pieces, lanes, by_y, page_owners):
    by_yz = lax.all_gather(by_y, DP[1], axis=1, tiled=False)
    gathered = by_yz.reshape((page_owners,) + by_y.shape[1:])
    parts = []
    start = 0
    for p in pieces:
        n = p.size // lanes
        parts.append(gathered[:, start : start + n])
        start += n
    return parts


def return_maxima(maxima):
    return lax.all_to_all(
        maxima.astype(jnp.bfloat16), DP, split_axis=0, concat_axis=0, tiled=True
    ).astype(maxima.dtype)


def body(
    hidden,
    query_weight,
    w_key,
    w_value,
    rel_table,
    rel_bucket,
    w_out,
    w_up,
    w_down,
    w_proj,
    pages,
    page_len,
    slot_per_page,
    candidates,
):
    qry_dev, qlen, width = hidden.shape
    heads_local = query_weight.shape[1] // HD
    cols = query_weight.shape[1]
    page_owners = lax.axis_size(DP)
    n_mp = lax.axis_size(MP)

    lanes = query_weight.shape[1]
    first = (query_weight, w_key, w_value, w_out.T, rel_table, w_proj)
    second = (w_up, w_down.T)
    first_y = gather_over_y(first, lanes)
    first_parts = gather_over_z(first, lanes, first_y, page_owners)
    pg_dev = pages.shape[0]
    ptok = pages.shape[1]
    ncand, ppc = (candidates.shape[1], candidates.shape[2])
    req = qry_dev * ncand * ppc
    cap = 2 * req // page_owners
    first_y, candidates = lax.optimization_barrier((first_y, candidates))
    slots = slot_per_page[candidates.reshape(req)]
    dest = slots // pg_dev
    local = slots % pg_dev
    query_of = jnp.arange(req, dtype=jnp.int32) // (ncand * ppc)
    member = (dest[:, None] == jnp.arange(page_owners, dtype=jnp.int32)[None, :]).astype(jnp.int32)
    place = jnp.sum((jnp.cumsum(member, axis=0) - 1) * member, axis=1)
    index = dest * cap + place
    codes = jnp.zeros((page_owners * cap,), jnp.int32).at[index].set(query_of * pg_dev + local)
    got = lax.all_to_all(codes.reshape(page_owners, cap), DP, split_axis=0, concat_axis=0, tiled=True)
    second_y = gather_over_y(second, lanes)
    first_parts, second_y, got = lax.optimization_barrier((first_parts, second_y, got))
    where_local = got % pg_dev
    which_query = got // pg_dev

    g_q, g_k, g_v, g_out, g_rel, g_proj = first_parts
    g_up, g_down = gather_over_z(second, lanes, second_y, page_owners)
    chosen = pages[where_local]
    lens = page_len[where_local]
    wq = g_q.reshape(page_owners * query_weight.shape[0], cols)
    wk = g_k.reshape(page_owners * w_key.shape[0], cols)
    wv = g_v.reshape(page_owners * w_value.shape[0], cols)
    wo = g_out.reshape(page_owners * w_out.shape[1], w_out.shape[0]).T
    wu = g_up.reshape(page_owners * w_up.shape[0], w_up.shape[1])
    wd = g_down.reshape(page_owners * w_down.shape[1], w_down.shape[0]).T
    left_rel = g_rel.reshape(page_owners * rel_table.shape[0], rel_table.shape[1])
    g_proj = g_proj.reshape((page_owners,) + w_proj.shape)

    spread = jnp.broadcast_to(hidden[None], (n_mp,) + hidden.shape)
    tokens = lax.all_to_all(spread, MP, split_axis=0, concat_axis=0, tiled=True)
    tokens = tokens.reshape((n_mp * qry_dev,) + hidden.shape[1:])
    group = tokens.shape[0]
    flat = tokens.reshape(group * qlen, width)
    qsum = add_rows(flat, wq)
    ksum = add_rows(flat, wk)
    vsum = add_rows(flat, wv)
    qrsum = add_rows(left_rel, wq)
    krsum = add_rows(left_rel, wk)
    rel_q = qrsum.astype(jnp.bfloat16)
    rel_k = krsum.astype(jnp.bfloat16)
    nbuck = rel_q.shape[0]
    qx = qsum.astype(jnp.bfloat16).reshape(group, qlen, heads_local, HD)
    kx = ksum.astype(jnp.bfloat16).reshape(group, qlen, heads_local, HD)
    vx = vsum.astype(jnp.bfloat16).reshape(group, qlen, heads_local, HD)
    rel_q = rel_q.reshape(nbuck, heads_local, HD)
    rel_k = rel_k.reshape(nbuck, heads_local, HD)
    onehot = (rel_bucket[:, :, None] == jnp.arange(nbuck, dtype=jnp.int32)[None, None, :]).astype(
        jnp.float32
    )
    scale = 1.0 / jnp.sqrt(jnp.float32(3 * HD))
    content = jnp.einsum("qihd,qjhd->qhij", qx, kx, preferred_element_type=jnp.float32)
    along_axis_name = jnp.einsum("qihd,bhd->qhib", qx, rel_k, preferred_element_type=jnp.float32)
    c2p = jnp.einsum("qhib,ijb->qhij", along_axis_name, onehot, precision=lax.Precision.HIGHEST)
    back = jnp.einsum("qjhd,bhd->qhjb", kx, rel_q, preferred_element_type=jnp.float32)
    p2c = jnp.einsum("qhjb,jib->qhij", back, onehot, precision=lax.Precision.HIGHEST)
    logits = (content + c2p + p2c) * scale
    probs = jax.nn.softmax(logits, axis=-1).astype(jnp.bfloat16)
    context_rows = jnp.einsum("qhij,qjhd->qihd", probs, vx, preferred_element_type=jnp.float32)
    context_rows = context_rows.astype(jnp.bfloat16).reshape(group * qlen, cols)
    attn_terms = jnp.dot(context_rows, wo, preferred_element_type=jnp.float32)
    attn = sum_to_owner(attn_terms, n_mp)
    own = hidden.reshape(qry_dev * qlen, width).astype(jnp.float32)
    mid = layer_norm(own + attn).astype(jnp.bfloat16)
    chosen, lens, mid = lax.optimization_barrier((chosen, lens, mid))
    both = jnp.concatenate([mid, g_proj.reshape(-1, mid.shape[1])], axis=0)
    both_all = lax.all_to_all(
        jnp.broadcast_to(both[None], (n_mp,) + both.shape), MP, split_axis=0, concat_axis=0, tiled=True
    )
    mid_all = both_all[:, : mid.shape[0]].reshape((n_mp * mid.shape[0], mid.shape[1]))
    proj_all = both_all[:, mid.shape[0] :].reshape((n_mp,) + g_proj.shape)
    wp = jnp.transpose(proj_all, (1, 0, 2, 3)).reshape(page_owners * n_mp * w_proj.shape[0], w_proj.shape[1])
    up = add_rows(mid_all, wu)
    inner = jax.nn.gelu(up, approximate=False).astype(jnp.bfloat16)
    down_terms = jnp.dot(inner, wd, preferred_element_type=jnp.float32)
    mlp = sum_to_owner(down_terms, n_mp)
    state = layer_norm(mid.astype(jnp.float32) + mlp).astype(jnp.bfloat16)
    width_out = w_proj.shape[1]
    proj = add_rows(state, wp)
    vectors = (proj / jnp.sqrt(jnp.sum(proj * proj, axis=-1, keepdims=True) + 1e-06)).astype(
        jnp.bfloat16
    )
    vectors = vectors.reshape(qry_dev, qlen, width_out)

    sent = jnp.broadcast_to(vectors[None], (page_owners, qry_dev, qlen, width_out))
    recv = lax.all_to_all(sent, DP, split_axis=0, concat_axis=0, tiled=True)
    token_positions = jnp.arange(ptok, dtype=jnp.int32)
    sim = jnp.einsum("sqie,snte->snqit", recv, chosen, preferred_element_type=jnp.float32)
    valid = token_positions[None, None, None, None, :] < lens[:, :, None, None, None]
    both_best = jnp.max(jnp.where(valid, sim, -1e30), axis=-1)
    picked = jnp.take_along_axis(both_best, which_query[:, :, None, None], axis=2)[:, :, 0]
    returned = return_maxima(picked)
    best = returned.reshape(page_owners * cap, qlen)[index]
    best = best.reshape(qry_dev, ncand, ppc, qlen)
    scores = jnp.sum(jnp.max(best, axis=2), axis=-1)
    return (vectors, scores)


def solution(mesh):
    in_specs = (
        P(DP + MP, None, None),
        P(DP, MP),
        P(DP, MP),
        P(DP, MP),
        P(DP, None),
        P(),
        P(MP, DP),
        P(DP, MP),
        P(MP, DP),
        P(DP + MP, None),
        P(DP, None, None),
        P(DP),
        P(),
        P(DP + MP, None, None),
    )
    out_specs = (P(DP + MP, None, None), P(DP + MP, None))
    fine = Mesh(mesh.devices.reshape(mesh.devices.shape[0] // 8, 8, mesh.devices.shape[1] // 2, 2), DP + MP)
    return jax.shard_map(body, mesh=fine, in_specs=in_specs, out_specs=out_specs, check_vma=False)
```

```python
import jax
import jax.numpy as jnp
from jax import lax
from jax.sharding import Mesh, PartitionSpec as P

HD = 64
DP = ("y", "z")
MP = ("x", "c")


def layer_norm(value):
    mean = jnp.mean(value, axis=-1, keepdims=True)
    centered = value - mean
    var = jnp.mean(centered * centered, axis=-1, keepdims=True)
    return centered / jnp.sqrt(var + 1e-07)


def add_rows(left, piece):
    return jnp.dot(left, piece, preferred_element_type=jnp.float32)


def sum_to_owner(terms, n_mp):
    pieces = terms.astype(jnp.bfloat16).reshape((n_mp, terms.shape[0] // n_mp) + terms.shape[1:])
    got = lax.all_to_all(pieces, MP, split_axis=0, concat_axis=0, tiled=True)
    return jnp.sum(got.astype(jnp.float32), axis=0).astype(jnp.bfloat16).astype(jnp.float32)


def gather_over_y(pieces, lanes):
    rows = sum(p.size // lanes for p in pieces)
    pad = jnp.zeros((-rows % 16, lanes), pieces[0].dtype)
    flat_pieces = jnp.concatenate([p.reshape(-1, lanes) for p in pieces] + [pad], axis=0)
    return lax.all_gather(flat_pieces, DP[0], axis=0, tiled=False)


def gather_over_z(pieces, lanes, by_y, page_owners):
    by_yz = lax.all_gather(by_y, DP[1], axis=1, tiled=False)
    gathered = by_yz.reshape((page_owners,) + by_y.shape[1:])
    parts = []
    start = 0
    for p in pieces:
        n = p.size // lanes
        parts.append(gathered[:, start : start + n])
        start += n
    return parts


def tile_order(piece, sub=8, lanes=128):
    rows, width = piece.shape
    tiles = piece.reshape(rows // sub, sub, width // lanes, lanes)
    return jnp.transpose(tiles, (0, 2, 1, 3)).reshape(-1, lanes)


def from_tile_order(gathered, shape, sub=8, lanes=128):
    rows, width = shape
    owners = gathered.shape[0]
    tiles = gathered.reshape(owners, rows // sub, width // lanes, sub, lanes)
    return jnp.transpose(tiles, (0, 1, 3, 2, 4)).reshape(owners * rows, width)


def return_maxima(maxima):
    return lax.all_to_all(
        maxima.astype(jnp.bfloat16), DP, split_axis=0, concat_axis=0, tiled=True
    ).astype(maxima.dtype)


def body(
    hidden,
    query_weight,
    w_key,
    w_value,
    rel_table,
    rel_bucket,
    w_out,
    w_up,
    w_down,
    w_proj,
    pages,
    page_len,
    slot_per_page,
    candidates,
):
    qry_dev, qlen, width = hidden.shape
    heads_local = query_weight.shape[1] // HD
    cols = query_weight.shape[1]
    page_owners = lax.axis_size(DP)
    n_mp = lax.axis_size(MP)

    lanes = query_weight.shape[1]
    first = (query_weight, w_key, w_value, w_out.T, rel_table, w_proj)
    second = (tile_order(w_up), tile_order(w_down.T))
    first_y = gather_over_y(first, lanes)
    first_parts = gather_over_z(first, lanes, first_y, page_owners)
    pg_dev = pages.shape[0]
    ptok = pages.shape[1]
    ncand, ppc = (candidates.shape[1], candidates.shape[2])
    req = qry_dev * ncand * ppc
    cap = 2 * req // page_owners
    first_y, candidates = lax.optimization_barrier((first_y, candidates))
    slots = slot_per_page[candidates.reshape(req)]
    dest = slots // pg_dev
    local = slots % pg_dev
    query_of = jnp.arange(req, dtype=jnp.int32) // (ncand * ppc)
    member = (dest[:, None] == jnp.arange(page_owners, dtype=jnp.int32)[None, :]).astype(jnp.int32)
    place = jnp.sum((jnp.cumsum(member, axis=0) - 1) * member, axis=1)
    index = dest * cap + place
    codes = jnp.zeros((page_owners * cap,), jnp.int32).at[index].set(query_of * pg_dev + local)
    got = lax.all_to_all(codes.reshape(page_owners, cap), DP, split_axis=0, concat_axis=0, tiled=True)
    second_y = gather_over_y(second, lanes)
    first_parts, second_y, got = lax.optimization_barrier((first_parts, second_y, got))
    where_local = got % pg_dev
    which_query = got // pg_dev

    g_q, g_k, g_v, g_out, g_rel, g_proj = first_parts
    g_up, g_down = gather_over_z(second, lanes, second_y, page_owners)
    chosen = pages[where_local]
    lens = page_len[where_local]
    wq = g_q.reshape(page_owners * query_weight.shape[0], cols)
    wk = g_k.reshape(page_owners * w_key.shape[0], cols)
    wv = g_v.reshape(page_owners * w_value.shape[0], cols)
    wo = g_out.reshape(page_owners * w_out.shape[1], w_out.shape[0]).T
    wu = from_tile_order(g_up, w_up.shape)
    wd = from_tile_order(g_down, (w_down.shape[1], w_down.shape[0])).T
    left_rel = g_rel.reshape(page_owners * rel_table.shape[0], rel_table.shape[1])
    g_proj = g_proj.reshape((page_owners,) + w_proj.shape)

    spread = jnp.broadcast_to(hidden[None], (n_mp,) + hidden.shape)
    tokens = lax.all_to_all(spread, MP, split_axis=0, concat_axis=0, tiled=True)
    tokens = tokens.reshape((n_mp * qry_dev,) + hidden.shape[1:])
    group = tokens.shape[0]
    flat = tokens.reshape(group * qlen, width)
    qsum = add_rows(flat, wq)
    ksum = add_rows(flat, wk)
    vsum = add_rows(flat, wv)
    qrsum = add_rows(left_rel, wq)
    krsum = add_rows(left_rel, wk)
    rel_q = qrsum.astype(jnp.bfloat16)
    rel_k = krsum.astype(jnp.bfloat16)
    nbuck = rel_q.shape[0]
    qx = qsum.astype(jnp.bfloat16).reshape(group, qlen, heads_local, HD)
    kx = ksum.astype(jnp.bfloat16).reshape(group, qlen, heads_local, HD)
    vx = vsum.astype(jnp.bfloat16).reshape(group, qlen, heads_local, HD)
    rel_q = rel_q.reshape(nbuck, heads_local, HD)
    rel_k = rel_k.reshape(nbuck, heads_local, HD)
    onehot = (rel_bucket[:, :, None] == jnp.arange(nbuck, dtype=jnp.int32)[None, None, :]).astype(
        jnp.float32
    )
    scale = 1.0 / jnp.sqrt(jnp.float32(3 * HD))
    content = jnp.einsum("qihd,qjhd->qhij", qx, kx, preferred_element_type=jnp.float32)
    along_axis_name = jnp.einsum("qihd,bhd->qhib", qx, rel_k, preferred_element_type=jnp.float32)
    c2p = jnp.einsum("qhib,ijb->qhij", along_axis_name, onehot, precision=lax.Precision.HIGHEST)
    back = jnp.einsum("qjhd,bhd->qhjb", kx, rel_q, preferred_element_type=jnp.float32)
    p2c = jnp.einsum("qhjb,jib->qhij", back, onehot, precision=lax.Precision.HIGHEST)
    logits = (content + c2p + p2c) * scale
    probs = jax.nn.softmax(logits, axis=-1).astype(jnp.bfloat16)
    context_rows = jnp.einsum("qhij,qjhd->qihd", probs, vx, preferred_element_type=jnp.float32)
    context_rows = context_rows.astype(jnp.bfloat16).reshape(group * qlen, cols)
    attn_terms = jnp.dot(context_rows, wo, preferred_element_type=jnp.float32)
    attn = sum_to_owner(attn_terms, n_mp)
    own = hidden.reshape(qry_dev * qlen, width).astype(jnp.float32)
    mid = layer_norm(own + attn).astype(jnp.bfloat16)
    chosen, lens, mid = lax.optimization_barrier((chosen, lens, mid))
    both = jnp.concatenate([mid, g_proj.reshape(-1, mid.shape[1])], axis=0)
    both_all = lax.all_to_all(
        jnp.broadcast_to(both[None], (n_mp,) + both.shape), MP, split_axis=0, concat_axis=0, tiled=True
    )
    mid_all = both_all[:, : mid.shape[0]].reshape((n_mp * mid.shape[0], mid.shape[1]))
    proj_all = both_all[:, mid.shape[0] :].reshape((n_mp,) + g_proj.shape)
    wp = jnp.transpose(proj_all, (1, 0, 2, 3)).reshape(page_owners * n_mp * w_proj.shape[0], w_proj.shape[1])
    up = add_rows(mid_all, wu)
    inner = jax.nn.gelu(up, approximate=False).astype(jnp.bfloat16)
    down_terms = jnp.dot(inner, wd, preferred_element_type=jnp.float32)
    mlp = sum_to_owner(down_terms, n_mp)
    state = layer_norm(mid.astype(jnp.float32) + mlp).astype(jnp.bfloat16)
    width_out = w_proj.shape[1]
    proj = add_rows(state, wp)
    vectors = (proj / jnp.sqrt(jnp.sum(proj * proj, axis=-1, keepdims=True) + 1e-06)).astype(
        jnp.bfloat16
    )
    vectors = vectors.reshape(qry_dev, qlen, width_out)

    sent = jnp.broadcast_to(vectors[None], (page_owners, qry_dev, qlen, width_out))
    recv = lax.all_to_all(sent, DP, split_axis=0, concat_axis=0, tiled=True)
    token_positions = jnp.arange(ptok, dtype=jnp.int32)
    sim = jnp.einsum("sqie,snte->snqit", recv, chosen, preferred_element_type=jnp.float32)
    valid = token_positions[None, None, None, None, :] < lens[:, :, None, None, None]
    both_best = jnp.max(jnp.where(valid, sim, -1e30), axis=-1)
    picked = jnp.where(which_query[:, :, None] == 0, both_best[:, :, 0], both_best[:, :, 1])
    returned = return_maxima(picked)
    best = returned.reshape(page_owners * cap, qlen)[index]
    best = best.reshape(qry_dev, ncand, ppc, qlen)
    scores = jnp.sum(jnp.max(best, axis=2), axis=-1)
    return (vectors, scores)


def solution(mesh):
    in_specs = (
        P(DP + MP, None, None),
        P(DP, MP),
        P(DP, MP),
        P(DP, MP),
        P(DP, None),
        P(),
        P(MP, DP),
        P(DP, MP),
        P(MP, DP),
        P(DP + MP, None),
        P(DP, None, None),
        P(DP),
        P(),
        P(DP + MP, None, None),
    )
    out_specs = (P(DP + MP, None, None), P(DP + MP, None))
    fine = Mesh(mesh.devices.reshape(mesh.devices.shape[0] // 8, 8, mesh.devices.shape[1] // 2, 2), DP + MP)
    return jax.shard_map(body, mesh=fine, in_specs=in_specs, out_specs=out_specs, check_vma=False)
```

```python
import jax
import jax.numpy as jnp
from jax import lax
from jax.sharding import Mesh, PartitionSpec as P

HD = 64
DP = ("y", "z")
MP = ("x", "c")


def layer_norm(value):
    mean = jnp.mean(value, axis=-1, keepdims=True)
    centered = value - mean
    var = jnp.mean(centered * centered, axis=-1, keepdims=True)
    return centered / jnp.sqrt(var + 1e-07)


def add_rows(left, piece):
    return jnp.dot(left, piece, preferred_element_type=jnp.float32)


def sum_to_owner(terms, n_mp):
    pieces = terms.astype(jnp.bfloat16).reshape((n_mp, terms.shape[0] // n_mp) + terms.shape[1:])
    got = lax.all_to_all(pieces, MP, split_axis=0, concat_axis=0, tiled=True)
    return jnp.sum(got.astype(jnp.float32), axis=0).astype(jnp.bfloat16).astype(jnp.float32)


def gather_over_y(pieces, lanes):
    rows = sum(p.size // lanes for p in pieces)
    pad = jnp.zeros((-rows % 16, lanes), pieces[0].dtype)
    flat_pieces = jnp.concatenate([p.reshape(-1, lanes) for p in pieces] + [pad], axis=0)
    return lax.all_gather(flat_pieces, DP[0], axis=0, tiled=False)


def gather_over_z(pieces, lanes, by_y, page_owners):
    by_yz = lax.all_gather(by_y, DP[1], axis=1, tiled=False)
    gathered = by_yz.reshape((page_owners,) + by_y.shape[1:])
    parts = []
    start = 0
    for p in pieces:
        n = p.size // lanes
        parts.append(gathered[:, start : start + n])
        start += n
    return parts


def tile_order(piece, sub=8, lanes=128):
    rows, width = piece.shape
    tiles = piece.reshape(rows // sub, sub, width // lanes, lanes)
    return jnp.transpose(tiles, (0, 2, 1, 3)).reshape(-1, lanes)


def from_tile_order(gathered, shape, sub=8, lanes=128):
    rows, width = shape
    owners = gathered.shape[0]
    tiles = gathered.reshape(owners, rows // sub, width // lanes, sub, lanes)
    return jnp.transpose(tiles, (0, 1, 3, 2, 4)).reshape(owners * rows, width)


def return_maxima(maxima):
    return lax.all_to_all(
        maxima.astype(jnp.bfloat16), DP, split_axis=0, concat_axis=0, tiled=True
    ).astype(maxima.dtype)


def body(
    hidden,
    query_weight,
    w_key,
    w_value,
    rel_table,
    rel_bucket,
    w_out,
    w_up,
    w_down,
    w_proj,
    pages,
    page_len,
    slot_per_page,
    candidates,
):
    qry_dev, qlen, width = hidden.shape
    heads_local = query_weight.shape[1] // HD
    cols = query_weight.shape[1]
    page_owners = lax.axis_size(DP)
    n_mp = lax.axis_size(MP)

    lanes = query_weight.shape[1]
    first = (query_weight, w_key, w_value, w_out.T, tile_order(rel_table), w_proj)
    second = (tile_order(w_up), tile_order(w_down.T))
    first_y = gather_over_y(first, lanes)
    first_parts = gather_over_z(first, lanes, first_y, page_owners)
    pg_dev = pages.shape[0]
    ptok = pages.shape[1]
    ncand, ppc = (candidates.shape[1], candidates.shape[2])
    req = qry_dev * ncand * ppc
    cap = 2 * req // page_owners
    first_y, candidates = lax.optimization_barrier((first_y, candidates))
    slots = slot_per_page[candidates.reshape(req)]
    dest = slots // pg_dev
    local = slots % pg_dev
    query_of = jnp.arange(req, dtype=jnp.int32) // (ncand * ppc)
    member = (dest[:, None] == jnp.arange(page_owners, dtype=jnp.int32)[None, :]).astype(jnp.int32)
    place = jnp.sum((jnp.cumsum(member, axis=0) - 1) * member, axis=1)
    index = dest * cap + place
    codes = jnp.zeros((page_owners * cap,), jnp.int32).at[index].set(query_of * pg_dev + local)
    got = lax.all_to_all(codes.reshape(page_owners, cap), DP, split_axis=0, concat_axis=0, tiled=True)
    second_y = gather_over_y(second, lanes)
    first_parts, second_y, got = lax.optimization_barrier((first_parts, second_y, got))
    where_local = got % pg_dev
    which_query = got // pg_dev

    g_q, g_k, g_v, g_out, g_rel, g_proj = first_parts
    g_up, g_down = gather_over_z(second, lanes, second_y, page_owners)
    chosen = pages[where_local]
    lens = page_len[where_local]
    wq = g_q.reshape(page_owners * query_weight.shape[0], cols)
    wk = g_k.reshape(page_owners * w_key.shape[0], cols)
    wv = g_v.reshape(page_owners * w_value.shape[0], cols)
    wo = g_out.reshape(page_owners * w_out.shape[1], w_out.shape[0]).T
    wu = from_tile_order(g_up, w_up.shape)
    wd = from_tile_order(g_down, (w_down.shape[1], w_down.shape[0])).T
    left_rel = from_tile_order(g_rel, rel_table.shape)
    g_proj = g_proj.reshape((page_owners,) + w_proj.shape)

    spread = jnp.broadcast_to(hidden[None], (n_mp,) + hidden.shape)
    tokens = lax.all_to_all(spread, MP, split_axis=0, concat_axis=0, tiled=True)
    tokens = tokens.reshape((n_mp * qry_dev,) + hidden.shape[1:])
    group = tokens.shape[0]
    flat = tokens.reshape(group * qlen, width)
    qsum = add_rows(flat, wq)
    ksum = add_rows(flat, wk)
    vsum = add_rows(flat, wv)
    qrsum = add_rows(left_rel, wq)
    krsum = add_rows(left_rel, wk)
    rel_q = qrsum.astype(jnp.bfloat16)
    rel_k = krsum.astype(jnp.bfloat16)
    nbuck = rel_q.shape[0]
    qx = qsum.astype(jnp.bfloat16).reshape(group, qlen, heads_local, HD)
    kx = ksum.astype(jnp.bfloat16).reshape(group, qlen, heads_local, HD)
    vx = vsum.astype(jnp.bfloat16).reshape(group, qlen, heads_local, HD)
    rel_q = rel_q.reshape(nbuck, heads_local, HD)
    rel_k = rel_k.reshape(nbuck, heads_local, HD)
    onehot = (rel_bucket[:, :, None] == jnp.arange(nbuck, dtype=jnp.int32)[None, None, :]).astype(
        jnp.float32
    )
    scale = 1.0 / jnp.sqrt(jnp.float32(3 * HD))
    content = jnp.einsum("qihd,qjhd->qhij", qx, kx, preferred_element_type=jnp.float32)
    along_axis_name = jnp.einsum("qihd,bhd->qhib", qx, rel_k, preferred_element_type=jnp.float32)
    c2p = jnp.einsum("qhib,ijb->qhij", along_axis_name, onehot, precision=lax.Precision.HIGHEST)
    back = jnp.einsum("qjhd,bhd->qhjb", kx, rel_q, preferred_element_type=jnp.float32)
    p2c = jnp.einsum("qhjb,jib->qhij", back, onehot, precision=lax.Precision.HIGHEST)
    logits = (content + c2p + p2c) * scale
    probs = jax.nn.softmax(logits, axis=-1).astype(jnp.bfloat16)
    context_rows = jnp.einsum("qhij,qjhd->qihd", probs, vx, preferred_element_type=jnp.float32)
    context_rows = context_rows.astype(jnp.bfloat16).reshape(group * qlen, cols)
    attn_terms = jnp.dot(context_rows, wo, preferred_element_type=jnp.float32)
    attn = sum_to_owner(attn_terms, n_mp)
    own = hidden.reshape(qry_dev * qlen, width).astype(jnp.float32)
    mid = layer_norm(own + attn).astype(jnp.bfloat16)
    chosen, lens, mid = lax.optimization_barrier((chosen, lens, mid))
    both = jnp.concatenate([mid, g_proj.reshape(-1, mid.shape[1])], axis=0)
    both_all = lax.all_to_all(
        jnp.broadcast_to(both[None], (n_mp,) + both.shape), MP, split_axis=0, concat_axis=0, tiled=True
    )
    mid_all = both_all[:, : mid.shape[0]].reshape((n_mp * mid.shape[0], mid.shape[1]))
    proj_all = both_all[:, mid.shape[0] :].reshape((n_mp,) + g_proj.shape)
    wp = jnp.transpose(proj_all, (1, 0, 2, 3)).reshape(page_owners * n_mp * w_proj.shape[0], w_proj.shape[1])
    up = add_rows(mid_all, wu)
    inner = jax.nn.gelu(up, approximate=False).astype(jnp.bfloat16)
    down_terms = jnp.dot(inner, wd, preferred_element_type=jnp.float32)
    mlp = sum_to_owner(down_terms, n_mp)
    state = layer_norm(mid.astype(jnp.float32) + mlp).astype(jnp.bfloat16)
    width_out = w_proj.shape[1]
    proj = add_rows(state, wp)
    vectors = (proj / jnp.sqrt(jnp.sum(proj * proj, axis=-1, keepdims=True) + 1e-06)).astype(
        jnp.bfloat16
    )
    vectors = vectors.reshape(qry_dev, qlen, width_out)

    sent = jnp.broadcast_to(vectors[None], (page_owners, qry_dev, qlen, width_out))
    recv = lax.all_to_all(sent, DP, split_axis=0, concat_axis=0, tiled=True)
    token_positions = jnp.arange(ptok, dtype=jnp.int32)
    sim = jnp.einsum("sqie,snte->snqit", recv, chosen, preferred_element_type=jnp.float32)
    valid = token_positions[None, None, None, None, :] < lens[:, :, None, None, None]
    both_best = jnp.max(jnp.where(valid, sim, -1e30), axis=-1)
    picked = jnp.where(which_query[:, :, None] == 0, both_best[:, :, 0], both_best[:, :, 1])
    returned = return_maxima(picked)
    best = returned.reshape(page_owners * cap, qlen)[index]
    best = best.reshape(qry_dev, ncand, ppc, qlen)
    scores = jnp.sum(jnp.max(best, axis=2), axis=-1)
    return (vectors, scores)


def solution(mesh):
    in_specs = (
        P(DP + MP, None, None),
        P(DP, MP),
        P(DP, MP),
        P(DP, MP),
        P(DP, None),
        P(),
        P(MP, DP),
        P(DP, MP),
        P(MP, DP),
        P(DP + MP, None),
        P(DP, None, None),
        P(DP),
        P(),
        P(DP + MP, None, None),
    )
    out_specs = (P(DP + MP, None, None), P(DP + MP, None))
    fine = Mesh(mesh.devices.reshape(mesh.devices.shape[0] // 8, 8, mesh.devices.shape[1] // 2, 2), DP + MP)
    return jax.shard_map(body, mesh=fine, in_specs=in_specs, out_specs=out_specs, check_vma=False)
```

```python
import jax
import jax.numpy as jnp
from jax import lax
from jax.sharding import Mesh, PartitionSpec as P

HD = 64
DP = ("y", "z")
MP = ("x", "c")


def layer_norm(value):
    mean = jnp.mean(value, axis=-1, keepdims=True)
    centered = value - mean
    var = jnp.mean(centered * centered, axis=-1, keepdims=True)
    return centered / jnp.sqrt(var + 1e-07)


def add_rows(left, piece):
    return jnp.dot(left, piece, preferred_element_type=jnp.float32)


def sum_to_owner(terms, n_mp):
    pieces = terms.astype(jnp.bfloat16).reshape((n_mp, terms.shape[0] // n_mp) + terms.shape[1:])
    got = lax.all_to_all(pieces, MP, split_axis=0, concat_axis=0, tiled=True)
    return jnp.sum(got.astype(jnp.float32), axis=0).astype(jnp.bfloat16).astype(jnp.float32)


def gather_over_y(pieces, lanes):
    rows = sum(p.size // lanes for p in pieces)
    pad = jnp.zeros((-rows % 16, lanes), pieces[0].dtype)
    flat_pieces = jnp.concatenate([p.reshape(-1, lanes) for p in pieces] + [pad], axis=0)
    return lax.all_gather(flat_pieces, DP[0], axis=0, tiled=False)


def gather_over_z(pieces, lanes, by_y, page_owners):
    by_yz = lax.all_gather(by_y, DP[1], axis=1, tiled=False)
    gathered = by_yz.reshape((page_owners,) + by_y.shape[1:])
    parts = []
    start = 0
    for p in pieces:
        n = p.size // lanes
        parts.append(gathered[:, start : start + n])
        start += n
    return parts


def tile_order(piece, sub=8, lanes=128):
    rows, width = piece.shape
    tiles = piece.reshape(rows // sub, sub, width // lanes, lanes)
    return jnp.transpose(tiles, (0, 2, 1, 3)).reshape(-1, lanes)


def from_tile_order(gathered, shape, sub=8, lanes=128):
    rows, width = shape
    owners = gathered.shape[0]
    tiles = gathered.reshape(owners, rows // sub, width // lanes, sub, lanes)
    return jnp.transpose(tiles, (0, 1, 3, 2, 4)).reshape(owners * rows, width)


def return_maxima(maxima):
    return lax.all_to_all(
        maxima.astype(jnp.bfloat16), DP, split_axis=0, concat_axis=0, tiled=True
    ).astype(maxima.dtype)


def body(
    hidden,
    query_weight,
    w_key,
    w_value,
    rel_table,
    rel_bucket,
    w_out,
    w_up,
    w_down,
    w_proj,
    pages,
    page_len,
    slot_per_page,
    candidates,
):
    qry_dev, qlen, width = hidden.shape
    heads_local = query_weight.shape[1] // HD
    cols = query_weight.shape[1]
    page_owners = lax.axis_size(DP)
    n_mp = lax.axis_size(MP)

    lanes = query_weight.shape[1]
    first = (query_weight, w_key, w_value, w_out.T, tile_order(rel_table), w_proj)
    second = (tile_order(w_up), tile_order(w_down.T))
    first_y = gather_over_y(first, lanes)
    first_parts = gather_over_z(first, lanes, first_y, page_owners)
    pg_dev = pages.shape[0]
    ptok = pages.shape[1]
    ncand, ppc = (candidates.shape[1], candidates.shape[2])
    req = qry_dev * ncand * ppc
    cap = 2 * req // page_owners
    first_y, candidates = lax.optimization_barrier((first_y, candidates))
    slots = slot_per_page[candidates.reshape(req)]
    dest = slots // pg_dev
    local = slots % pg_dev
    query_of = jnp.arange(req, dtype=jnp.int32) // (ncand * ppc)
    member = (dest[:, None] == jnp.arange(page_owners, dtype=jnp.int32)[None, :]).astype(jnp.int32)
    place = jnp.sum((jnp.cumsum(member, axis=0) - 1) * member, axis=1)
    index = dest * cap + place
    codes = jnp.zeros((page_owners * cap,), jnp.int32).at[index].set(query_of * pg_dev + local)
    got = lax.all_to_all(codes.reshape(page_owners, cap), DP, split_axis=0, concat_axis=0, tiled=True)
    second_y = lax.all_gather(jnp.stack(second), DP[0], axis=1, tiled=False)
    first_parts, second_y, got = lax.optimization_barrier((first_parts, second_y, got))
    where_local = got % pg_dev
    which_query = got // pg_dev

    g_q, g_k, g_v, g_out, g_rel, g_proj = first_parts
    second_all = lax.all_gather(second_y, DP[1], axis=2, tiled=False)
    second_all = second_all.reshape((len(second), page_owners) + second[0].shape)
    g_up, g_down = second_all[0], second_all[1]
    chosen = pages[where_local]
    lens = page_len[where_local]
    wq = g_q.reshape(page_owners * query_weight.shape[0], cols)
    wk = g_k.reshape(page_owners * w_key.shape[0], cols)
    wv = g_v.reshape(page_owners * w_value.shape[0], cols)
    wo = g_out.reshape(page_owners * w_out.shape[1], w_out.shape[0]).T
    wu = from_tile_order(g_up, w_up.shape)
    wd = from_tile_order(g_down, (w_down.shape[1], w_down.shape[0])).T
    left_rel = from_tile_order(g_rel, rel_table.shape)
    g_proj = g_proj.reshape((page_owners,) + w_proj.shape)

    spread = jnp.broadcast_to(hidden[None], (n_mp,) + hidden.shape)
    tokens = lax.all_to_all(spread, MP, split_axis=0, concat_axis=0, tiled=True)
    tokens = tokens.reshape((n_mp * qry_dev,) + hidden.shape[1:])
    group = tokens.shape[0]
    flat = tokens.reshape(group * qlen, width)
    qsum = add_rows(flat, wq)
    ksum = add_rows(flat, wk)
    vsum = add_rows(flat, wv)
    qrsum = add_rows(left_rel, wq)
    krsum = add_rows(left_rel, wk)
    rel_q = qrsum.astype(jnp.bfloat16)
    rel_k = krsum.astype(jnp.bfloat16)
    nbuck = rel_q.shape[0]
    qx = qsum.astype(jnp.bfloat16).reshape(group, qlen, heads_local, HD)
    kx = ksum.astype(jnp.bfloat16).reshape(group, qlen, heads_local, HD)
    vx = vsum.astype(jnp.bfloat16).reshape(group, qlen, heads_local, HD)
    rel_q = rel_q.reshape(nbuck, heads_local, HD)
    rel_k = rel_k.reshape(nbuck, heads_local, HD)
    onehot = (rel_bucket[:, :, None] == jnp.arange(nbuck, dtype=jnp.int32)[None, None, :]).astype(
        jnp.float32
    )
    scale = 1.0 / jnp.sqrt(jnp.float32(3 * HD))
    content = jnp.einsum("qihd,qjhd->qhij", qx, kx, preferred_element_type=jnp.float32)
    along_axis_name = jnp.einsum("qihd,bhd->qhib", qx, rel_k, preferred_element_type=jnp.float32)
    c2p = jnp.einsum("qhib,ijb->qhij", along_axis_name, onehot, precision=lax.Precision.HIGHEST)
    back = jnp.einsum("qjhd,bhd->qhjb", kx, rel_q, preferred_element_type=jnp.float32)
    p2c = jnp.einsum("qhjb,jib->qhij", back, onehot, precision=lax.Precision.HIGHEST)
    logits = (content + c2p + p2c) * scale
    probs = jax.nn.softmax(logits, axis=-1).astype(jnp.bfloat16)
    context_rows = jnp.einsum("qhij,qjhd->qihd", probs, vx, preferred_element_type=jnp.float32)
    context_rows = context_rows.astype(jnp.bfloat16).reshape(group * qlen, cols)
    attn_terms = jnp.dot(context_rows, wo, preferred_element_type=jnp.float32)
    attn = sum_to_owner(attn_terms, n_mp)
    own = hidden.reshape(qry_dev * qlen, width).astype(jnp.float32)
    mid = layer_norm(own + attn).astype(jnp.bfloat16)
    chosen, lens, mid = lax.optimization_barrier((chosen, lens, mid))
    both = jnp.concatenate([mid, g_proj.reshape(-1, mid.shape[1])], axis=0)
    both_all = lax.all_to_all(
        jnp.broadcast_to(both[None], (n_mp,) + both.shape), MP, split_axis=0, concat_axis=0, tiled=True
    )
    mid_all = both_all[:, : mid.shape[0]].reshape((n_mp * mid.shape[0], mid.shape[1]))
    proj_all = both_all[:, mid.shape[0] :].reshape((n_mp,) + g_proj.shape)
    wp = jnp.transpose(proj_all, (1, 0, 2, 3)).reshape(page_owners * n_mp * w_proj.shape[0], w_proj.shape[1])
    up = add_rows(mid_all, wu)
    inner = jax.nn.gelu(up, approximate=False).astype(jnp.bfloat16)
    down_terms = jnp.dot(inner, wd, preferred_element_type=jnp.float32)
    mlp = sum_to_owner(down_terms, n_mp)
    state = layer_norm(mid.astype(jnp.float32) + mlp).astype(jnp.bfloat16)
    width_out = w_proj.shape[1]
    proj = add_rows(state, wp)
    vectors = (proj / jnp.sqrt(jnp.sum(proj * proj, axis=-1, keepdims=True) + 1e-06)).astype(
        jnp.bfloat16
    )
    vectors = vectors.reshape(qry_dev, qlen, width_out)

    sent = jnp.broadcast_to(vectors[None], (page_owners, qry_dev, qlen, width_out))
    recv = lax.all_to_all(sent, DP, split_axis=0, concat_axis=0, tiled=True)
    token_positions = jnp.arange(ptok, dtype=jnp.int32)
    sim = jnp.einsum("sqie,snte->snqit", recv, chosen, preferred_element_type=jnp.float32)
    valid = token_positions[None, None, None, None, :] < lens[:, :, None, None, None]
    both_best = jnp.max(jnp.where(valid, sim, -1e30), axis=-1)
    picked = jnp.where(which_query[:, :, None] == 0, both_best[:, :, 0], both_best[:, :, 1])
    returned = return_maxima(picked)
    best = returned.reshape(page_owners * cap, qlen)[index]
    best = best.reshape(qry_dev, ncand, ppc, qlen)
    scores = jnp.sum(jnp.max(best, axis=2), axis=-1)
    return (vectors, scores)


def solution(mesh):
    in_specs = (
        P(DP + MP, None, None),
        P(DP, MP),
        P(DP, MP),
        P(DP, MP),
        P(DP, None),
        P(),
        P(MP, DP),
        P(DP, MP),
        P(MP, DP),
        P(DP + MP, None),
        P(DP, None, None),
        P(DP),
        P(),
        P(DP + MP, None, None),
    )
    out_specs = (P(DP + MP, None, None), P(DP + MP, None))
    fine = Mesh(mesh.devices.reshape(mesh.devices.shape[0] // 8, 8, mesh.devices.shape[1] // 2, 2), DP + MP)
    return jax.shard_map(body, mesh=fine, in_specs=in_specs, out_specs=out_specs, check_vma=False)
```

```python
import jax
import jax.numpy as jnp
from jax import lax
from jax.sharding import Mesh, PartitionSpec as P

HD = 64
DP = ("y", "z")
MP = ("x", "c")


def layer_norm(value):
    mean = jnp.mean(value, axis=-1, keepdims=True)
    centered = value - mean
    var = jnp.mean(centered * centered, axis=-1, keepdims=True)
    return centered / jnp.sqrt(var + 1e-07)


def add_rows(left, piece):
    return jnp.dot(left, piece, preferred_element_type=jnp.float32)


def sum_to_owner(terms, n_mp):
    pieces = terms.astype(jnp.bfloat16).reshape((n_mp, terms.shape[0] // n_mp) + terms.shape[1:])
    got = lax.all_to_all(pieces, MP, split_axis=0, concat_axis=0, tiled=True)
    return jnp.sum(got.astype(jnp.float32), axis=0)


def gather_over_y(pieces, lanes):
    rows = sum(p.size // lanes for p in pieces)
    pad = jnp.zeros((-rows % 16, lanes), pieces[0].dtype)
    flat_pieces = jnp.concatenate([p.reshape(-1, lanes) for p in pieces] + [pad], axis=0)
    return lax.all_gather(flat_pieces, DP[0], axis=0, tiled=False)


def gather_over_z(pieces, lanes, by_y, page_owners):
    by_yz = lax.all_gather(by_y, DP[1], axis=1, tiled=False)
    gathered = by_yz.reshape((page_owners,) + by_y.shape[1:])
    parts = []
    start = 0
    for p in pieces:
        n = p.size // lanes
        parts.append(gathered[:, start : start + n])
        start += n
    return parts


def tile_order(piece, sub=8, lanes=128):
    rows, width = piece.shape
    tiles = piece.reshape(rows // sub, sub, width // lanes, lanes)
    return jnp.transpose(tiles, (0, 2, 1, 3)).reshape(-1, lanes)


def from_tile_order(gathered, shape, sub=8, lanes=128):
    rows, width = shape
    owners = gathered.shape[0]
    tiles = gathered.reshape(owners, rows // sub, width // lanes, sub, lanes)
    return jnp.transpose(tiles, (0, 1, 3, 2, 4)).reshape(owners * rows, width)


def return_maxima(maxima):
    return lax.all_to_all(
        maxima.astype(jnp.bfloat16), DP, split_axis=0, concat_axis=0, tiled=True
    ).astype(maxima.dtype)


def body(
    hidden,
    query_weight,
    w_key,
    w_value,
    rel_table,
    rel_bucket,
    w_out,
    w_up,
    w_down,
    w_proj,
    pages,
    page_len,
    slot_per_page,
    candidates,
):
    qry_dev, qlen, width = hidden.shape
    heads_local = query_weight.shape[1] // HD
    cols = query_weight.shape[1]
    page_owners = lax.axis_size(DP)
    n_mp = lax.axis_size(MP)

    lanes = query_weight.shape[1]
    first = (query_weight, w_key, w_value, w_out.T, tile_order(rel_table), w_proj)
    second = (tile_order(w_up), tile_order(w_down.T))
    first_y = gather_over_y(first, lanes)
    first_parts = gather_over_z(first, lanes, first_y, page_owners)
    pg_dev = pages.shape[0]
    ptok = pages.shape[1]
    ncand, ppc = (candidates.shape[1], candidates.shape[2])
    req = qry_dev * ncand * ppc
    cap = 2 * req // page_owners
    first_y, candidates = lax.optimization_barrier((first_y, candidates))
    slots = slot_per_page[candidates.reshape(req)]
    dest = slots // pg_dev
    local = slots % pg_dev
    query_of = jnp.arange(req, dtype=jnp.int32) // (ncand * ppc)
    member = (dest[:, None] == jnp.arange(page_owners, dtype=jnp.int32)[None, :]).astype(jnp.int32)
    place = jnp.sum((jnp.cumsum(member, axis=0) - 1) * member, axis=1)
    index = dest * cap + place
    codes = jnp.zeros((page_owners * cap,), jnp.int32).at[index].set(query_of * pg_dev + local)
    got = lax.all_to_all(codes.reshape(page_owners, cap), DP, split_axis=0, concat_axis=0, tiled=True)
    second_y = lax.all_gather(jnp.stack(second), DP[0], axis=1, tiled=False)
    first_parts, second_y, got = lax.optimization_barrier((first_parts, second_y, got))
    where_local = got % pg_dev
    which_query = got // pg_dev

    g_q, g_k, g_v, g_out, g_rel, g_proj = first_parts
    second_all = lax.all_gather(second_y, DP[1], axis=2, tiled=False)
    second_all = second_all.reshape((len(second), page_owners) + second[0].shape)
    g_up, g_down = second_all[0], second_all[1]
    chosen = pages[where_local]
    lens = page_len[where_local]
    wq = g_q.reshape(page_owners * query_weight.shape[0], cols)
    wk = g_k.reshape(page_owners * w_key.shape[0], cols)
    wv = g_v.reshape(page_owners * w_value.shape[0], cols)
    wo = g_out.reshape(page_owners * w_out.shape[1], w_out.shape[0]).T
    wu = from_tile_order(g_up, w_up.shape)
    wd = from_tile_order(g_down, (w_down.shape[1], w_down.shape[0])).T
    left_rel = from_tile_order(g_rel, rel_table.shape)
    g_proj = g_proj.reshape((page_owners,) + w_proj.shape)

    spread = jnp.broadcast_to(hidden[None], (n_mp,) + hidden.shape)
    tokens = lax.all_to_all(spread, MP, split_axis=0, concat_axis=0, tiled=True)
    tokens = tokens.reshape((n_mp * qry_dev,) + hidden.shape[1:])
    group = tokens.shape[0]
    flat = tokens.reshape(group * qlen, width)
    qsum = add_rows(flat, wq)
    ksum = add_rows(flat, wk)
    vsum = add_rows(flat, wv)
    qrsum = add_rows(left_rel, wq)
    krsum = add_rows(left_rel, wk)
    rel_q = qrsum.astype(jnp.bfloat16)
    rel_k = krsum.astype(jnp.bfloat16)
    nbuck = rel_q.shape[0]
    qx = qsum.astype(jnp.bfloat16).reshape(group, qlen, heads_local, HD)
    kx = ksum.astype(jnp.bfloat16).reshape(group, qlen, heads_local, HD)
    vx = vsum.astype(jnp.bfloat16).reshape(group, qlen, heads_local, HD)
    rel_q = rel_q.reshape(nbuck, heads_local, HD)
    rel_k = rel_k.reshape(nbuck, heads_local, HD)
    onehot = (rel_bucket[:, :, None] == jnp.arange(nbuck, dtype=jnp.int32)[None, None, :]).astype(
        jnp.float32
    )
    scale = 1.0 / jnp.sqrt(jnp.float32(3 * HD))
    content = jnp.einsum("qihd,qjhd->qhij", qx, kx, preferred_element_type=jnp.float32)
    along_axis_name = jnp.einsum("qihd,bhd->qhib", qx, rel_k, preferred_element_type=jnp.float32)
    c2p = jnp.einsum("qhib,ijb->qhij", along_axis_name, onehot, precision=lax.Precision.HIGHEST)
    back = jnp.einsum("qjhd,bhd->qhjb", kx, rel_q, preferred_element_type=jnp.float32)
    p2c = jnp.einsum("qhjb,jib->qhij", back, onehot, precision=lax.Precision.HIGHEST)
    logits = (content + c2p + p2c) * scale
    probs = jax.nn.softmax(logits, axis=-1).astype(jnp.bfloat16)
    context_rows = jnp.einsum("qhij,qjhd->qihd", probs, vx, preferred_element_type=jnp.float32)
    context_rows = context_rows.astype(jnp.bfloat16).reshape(group * qlen, cols)
    attn_terms = jnp.dot(context_rows, wo, preferred_element_type=jnp.float32)
    attn = sum_to_owner(attn_terms, n_mp)
    own = hidden.reshape(qry_dev * qlen, width).astype(jnp.float32)
    mid = layer_norm(own + attn).astype(jnp.bfloat16)
    chosen, lens, mid = lax.optimization_barrier((chosen, lens, mid))
    both = jnp.concatenate([mid, g_proj.reshape(-1, mid.shape[1])], axis=0)
    both_all = lax.all_to_all(
        jnp.broadcast_to(both[None], (n_mp,) + both.shape), MP, split_axis=0, concat_axis=0, tiled=True
    )
    mid_all = both_all[:, : mid.shape[0]].reshape((n_mp * mid.shape[0], mid.shape[1]))
    proj_all = both_all[:, mid.shape[0] :].reshape((n_mp,) + g_proj.shape)
    wp = jnp.transpose(proj_all, (1, 0, 2, 3)).reshape(page_owners * n_mp * w_proj.shape[0], w_proj.shape[1])
    up = add_rows(mid_all, wu)
    inner = jax.nn.gelu(up, approximate=False).astype(jnp.bfloat16)
    down_terms = jnp.dot(inner, wd, preferred_element_type=jnp.float32)
    mlp = sum_to_owner(down_terms, n_mp)
    state = layer_norm(mid.astype(jnp.float32) + mlp).astype(jnp.bfloat16)
    width_out = w_proj.shape[1]
    proj = add_rows(state, wp)
    vectors = (proj / jnp.sqrt(jnp.sum(proj * proj, axis=-1, keepdims=True) + 1e-06)).astype(
        jnp.bfloat16
    )
    vectors = vectors.reshape(qry_dev, qlen, width_out)

    sent = jnp.broadcast_to(vectors[None], (page_owners, qry_dev, qlen, width_out))
    recv = lax.all_to_all(sent, DP, split_axis=0, concat_axis=0, tiled=True)
    token_positions = jnp.arange(ptok, dtype=jnp.int32)
    sim = jnp.einsum("sqie,snte->snqit", recv, chosen, preferred_element_type=jnp.float32)
    valid = token_positions[None, None, None, None, :] < lens[:, :, None, None, None]
    both_best = jnp.max(jnp.where(valid, sim, -1e30), axis=-1)
    picked = jnp.where(which_query[:, :, None] == 0, both_best[:, :, 0], both_best[:, :, 1])
    returned = return_maxima(picked)
    best = returned.reshape(page_owners * cap, qlen)[index]
    best = best.reshape(qry_dev, ncand, ppc, qlen)
    scores = jnp.sum(jnp.max(best, axis=2), axis=-1)
    return (vectors, scores)


def solution(mesh):
    in_specs = (
        P(DP + MP, None, None),
        P(DP, MP),
        P(DP, MP),
        P(DP, MP),
        P(DP, None),
        P(),
        P(MP, DP),
        P(DP, MP),
        P(MP, DP),
        P(DP + MP, None),
        P(DP, None, None),
        P(DP),
        P(),
        P(DP + MP, None, None),
    )
    out_specs = (P(DP + MP, None, None), P(DP + MP, None))
    fine = Mesh(mesh.devices.reshape(mesh.devices.shape[0] // 8, 8, mesh.devices.shape[1] // 2, 2), DP + MP)
    return jax.shard_map(body, mesh=fine, in_specs=in_specs, out_specs=out_specs, check_vma=False)
```
